128 devices in a mesh: dp: 4 (over x_hi, core), mp: 32 (over z, x_lo, y).
Axes of the slice: x: 4 (x_hi: 2, x_lo: 2; x = x_hi * 2 + x_lo), y: 4, z: 4, core: 2. Of those that a mesh axis runs over, the one named last changes fastest.
Arguments:
- prompt_rows: bfloat16 [65536, 2048], P(('dp', 'mp')), may hold values from -6 to 6
- step_rows: bfloat16 [16, 2048], P('dp', 'mp'), may hold values from -6 to 6
- attn_gain: float32 [2048], replicated, may hold values from 0.1 to 1.9
- latent_gain: float32 [512], replicated, may hold values from 0.1 to 1.9
- joined_qkva: float32 [2048, 3648], P('dp', 'mp'), may hold values from -2.4748737 to 2.4748737
- kv_up: float32 [512, 4096], P('dp', 'mp'), may hold values from -0.25 to 0.25
- out_proj: float32 [2048, 2048], P('dp', 'mp'), may hold values from -1.5 to 1.5
- latent_cache: bfloat16 [256, 16, 576], P(('dp', 'mp')), may hold values from -6 to 6
- page_table: int32 [16, 8], P('dp'), may hold values from 0 to 63, as said below
- cached_lengths: int32 [16], P('dp'), may hold values from 1 to 127, as said below
Outputs:
- prompt_out: bfloat16 [65536, 2048], P(('dp', 'mp'))
- step_out: bfloat16 [16, 2048], P('dp', 'mp')
The draws below stay inside these ranges and needn't reach their ends.
Inputs may be any that keep to these rules, and one draw needn't show every extreme that they name: `page_table`: row r lists the slots of r's 8 pages, numbered within the pool of r's index of dp; slot g lies on index g // 2 of mp. No slot is listed twice within one index of dp. `cached_lengths`: some request has 127 cached tokens and some has one.
All inputs are finite; a program needn't handle non-finite values.
Results may differ from the reference program's by a relative error of at most 0.015.
Values may be sent and summed in bfloat16 or wider, within the bound.
No kernel may reach another device: no remote copies, remote signals or barrier semaphores. Data moves between devices by JAX's collectives and lax.ppermute only.
A program may use at most 128 MiB of HBM per device.

```python
import math
import jax
import jax.numpy as jnp
from jax import lax

D = 2048
H = 16
DN = 128
DR = 64
DV = 128
LAT = 512
LEN = 512
PAGE = 16
CTX = 128
REQ_GRP = 4
JOINED = 3648
UPCOLS = 4096
HEADOUT = 2048
KEYW = 576
PAGES_REQ = 8
GROUP_POOL = 64
TOKENS = 65536
REQS = 16
POOL_ALL = 256
N_DP = 4


def draw_joined_qkva(key, part):
    base_key = jax.random.fold_in(jax.random.fold_in(key, 17), 0)
    base = jax.random.normal(base_key, (D, JOINED), jnp.float32)
    return jnp.clip(base, -6.0, 6.0) * D ** (-0.5)


def draw_page_table(key, part):
    group_count = REQS // REQ_GRP
    taken_count = REQ_GRP * PAGES_REQ

    def one_group(group_key):
        chosen = jax.random.permutation(group_key, GROUP_POOL)[:taken_count]
        chosen = jnp.where(chosen == jnp.max(chosen), GROUP_POOL - 1, chosen)
        chosen = jnp.where(chosen == jnp.min(chosen), 0, chosen)
        return chosen.reshape(REQ_GRP, PAGES_REQ)
    tables = jax.vmap(one_group)(jax.random.split(key, group_count))
    return tables.reshape(REQS, PAGES_REQ).astype(jnp.int32)


def draw_cached_lengths(key, part):
    length_key, place_key = jax.random.split(key)
    lengths = jax.random.randint(length_key, (REQS,), 1, CTX)
    picked = jax.random.permutation(place_key, REQS)
    lengths = lengths.at[picked[0]].set(CTX - 1)
    lengths = lengths.at[picked[1]].set(1)
    return lengths.astype(jnp.int32)


def level_of(rng, extent, cuts, low, high):
    gain, own = 1.0, jax.random.fold_in(rng, 6)
    for axis_at, parts in cuts:
        steps = jnp.exp(jax.random.uniform(jax.random.fold_in(own, axis_at), (parts,), jnp.float32, low / len(cuts), high / len(cuts)))
        gain = gain * jnp.repeat(steps, extent[axis_at] // parts).reshape([-1 if axis == axis_at else 1 for axis in range(len(extent))])
    return gain


def normal_values(rng, dims, width, reach, shards=(), kind=jnp.bfloat16):
    factor_of = level_of(rng, dims, shards, -0.22, 0.18) if shards else 1.0
    entries = jax.random.normal(rng, dims, jnp.float32) * width * factor_of
    return jnp.minimum(jnp.maximum(entries, -reach), reach).astype(kind)


def setup_inputs(seed: int = 0) -> dict:
    keys = jax.random.split(jax.random.key(seed), 11)
    return {
        "prompt_rows": normal_values(keys[0], (TOKENS, D), 1.0, 6.0, ((0, 128),)),
        "step_rows": normal_values(keys[1], (REQS, D), 1.0, 6.0, ((0, 4), (1, 32))),
        "attn_gain": jnp.clip(1.0 + 0.18 * jax.random.normal(keys[2], (D,), jnp.float32), 0.1, 1.9),
        "latent_gain": jnp.clip(1.0 + 0.18 * jax.random.normal(keys[3], (LAT,), jnp.float32), 0.1, 1.9),
        "joined_qkva": draw_joined_qkva(jax.random.fold_in(keys[10], 71), 0),
        "kv_up": normal_values(keys[5], (LAT, UPCOLS), LAT ** -0.5, 0.25, ((0, 4), (1, 32)), jnp.float32),
        "out_proj": normal_values(keys[6], (HEADOUT, D), H ** -0.5, 1.5, ((0, 4), (1, 32)), jnp.float32),
        "latent_cache": normal_values(keys[7], (POOL_ALL, PAGE, KEYW), 1.0, 6.0, ((0, 128),)),
        "page_table": draw_page_table(jax.random.fold_in(keys[10], 71), 0),
        "cached_lengths": draw_cached_lengths(jax.random.fold_in(keys[10], 71), 0),
    }


NORM_EPS = 1e-06
ROPE_BASE = 50000.0
MASKED = -1e+30

def rms_scale(values, scales):
    widened = values.astype(jnp.float32)
    mean_square = lax.optimization_barrier(jnp.mean(widened * widened, axis=-1, keepdims=True))
    return widened * lax.rsqrt(mean_square + NORM_EPS) * scales

def rotate(values, positions):
    rot_width = values.shape[-1]
    half_width = rot_width // 2
    freq_steps = jnp.arange(half_width, dtype=jnp.float32)
    inv_freqs = jnp.exp(freq_steps * (-2.0 * math.log(ROPE_BASE) / rot_width))
    angles = positions.astype(jnp.float32)[:, None] * inv_freqs[None, :]
    angle_shape = (positions.shape[0],) + (1,) * (values.ndim - 2) + (half_width,)
    cosine = jnp.cos(angles).reshape(angle_shape)
    sine_part = jnp.sin(angles).reshape(angle_shape)
    lower_half = values[..., :half_width]
    upper_half = values[..., half_width:]
    return jnp.concatenate([lower_half * cosine - upper_half * sine_part, upper_half * cosine + lower_half * sine_part], axis=-1)

def attend(queries, key_rows, allowed, score_scale):
    scores = jnp.einsum('qhc,kc->qhk', queries.astype(jnp.float32), key_rows.astype(jnp.float32)) * score_scale
    scores = jnp.where(allowed[:, None, :], scores, MASKED)
    peak_score = lax.optimization_barrier(jnp.max(scores, axis=-1, keepdims=True))
    weights = jnp.where(allowed[:, None, :], jnp.exp(scores - peak_score), 0.0)
    weight_sum = lax.optimization_barrier(jnp.sum(weights, axis=-1, keepdims=True))
    half_weights = lax.optimization_barrier(weights.astype(jnp.bfloat16)).astype(jnp.float32)
    summed = jnp.einsum('qhk,kl->qhl', half_weights, key_rows[:, :LAT].astype(jnp.float32))
    return (summed / weight_sum).astype(jnp.bfloat16)

def reference(prompt_rows, step_rows, attn_gain, latent_gain, joined_qkva, kv_up, out_proj, latent_cache, page_table, cached_lengths):
    score_scale = (DN + DR) ** (-0.5)
    w_joined = joined_qkva.astype(jnp.bfloat16)
    w_up = kv_up.astype(jnp.bfloat16)
    w_output = out_proj.astype(jnp.bfloat16)
    up_heads = w_up.reshape(LAT, H, DN + DV)
    head_cols = H * (DN + DR)

    def queries_keys(source_rows, positions):
        normed = rms_scale(source_rows, attn_gain).astype(jnp.bfloat16)
        projected = jnp.dot(normed, w_joined, preferred_element_type=jnp.float32).astype(jnp.bfloat16)
        row_count = projected.shape[0]
        query_cols = projected[:, :head_cols].reshape(row_count, H, DN + DR)
        query_rot = rotate(query_cols[..., DN:].astype(jnp.float32), positions).astype(jnp.bfloat16)
        latent = rms_scale(projected[:, head_cols:head_cols + LAT], latent_gain).astype(jnp.bfloat16)
        key_rot = rotate(projected[:, head_cols + LAT:].astype(jnp.float32), positions).astype(jnp.bfloat16)
        query_lat = jnp.einsum('rhn,lhn->rhl', query_cols[..., :DN].astype(jnp.float32), up_heads[..., :DN].astype(jnp.float32)).astype(jnp.bfloat16)
        queries = jnp.concatenate([query_lat, query_rot], axis=-1)
        key_rows = jnp.concatenate([latent, key_rot], axis=-1)
        return (queries, key_rows)

    def finish(latent_out):
        heads_out = jnp.einsum('rhl,lhv->rhv', latent_out.astype(jnp.float32), up_heads[..., DN:].astype(jnp.float32)).astype(jnp.bfloat16)
        heads_out = heads_out.reshape(latent_out.shape[0], H * DV)
        return jnp.dot(heads_out, w_output, preferred_element_type=jnp.float32).astype(jnp.bfloat16)

    def one_prompt(tokens):
        positions = jnp.arange(LEN, dtype=jnp.int32)
        queries, key_rows = queries_keys(tokens, positions)
        allowed = positions[None, :] <= positions[:, None]
        return finish(attend(queries, key_rows, allowed, score_scale))
    prompt_out = lax.map(one_prompt, prompt_rows.reshape(-1, LEN, D)).reshape(-1, D)
    queries, key_rows = queries_keys(step_rows, cached_lengths)
    cache_groups = latent_cache.reshape(N_DP, GROUP_POOL, PAGE, LAT + DR)
    group_ids = jnp.arange(REQS, dtype=jnp.int32) // REQ_GRP
    pages = cache_groups[group_ids[:, None], page_table].reshape(REQS, CTX, LAT + DR)
    key_all = jnp.concatenate([pages, key_rows[:, None, :]], axis=1)
    cached_ok = jnp.arange(CTX, dtype=jnp.int32)[None, :] < cached_lengths[:, None]
    allowed_all = jnp.concatenate([cached_ok, jnp.ones((REQS, 1), dtype=jnp.bool_)], axis=1)

    def one_request(query_one, key_one, allowed_one):
        return attend(query_one[None], key_one, allowed_one[None], score_scale)[0]
    step_latent = jax.vmap(one_request)(queries, key_all, allowed_all)
    step_out = finish(step_latent)
    return (prompt_out, step_out)
```

```python
import math

import jax
import jax.numpy as jnp
from jax import lax
from jax.sharding import PartitionSpec as P

H = 16
DN = 128
DR = 64
DV = 128
LAT = 512
LEN = 512


NORM_EPS = 1e-06
ROPE_BASE = 50000.0
MASKED = -1e30


def gather_weight(block):
    rows = lax.all_gather(block.astype(jnp.bfloat16), "dp", axis=0, tiled=True)
    return lax.all_gather(rows, "mp", axis=1, tiled=True)


def rms_scale(values, scales):
    widened = values.astype(jnp.float32)
    mean_square = jnp.mean(widened * widened, axis=-1, keepdims=True)
    return widened * lax.rsqrt(mean_square + NORM_EPS) * scales


def rotate(values, positions):
    rot_width = values.shape[-1]
    half_width = rot_width // 2
    freq_steps = jnp.arange(half_width, dtype=jnp.float32)
    inv_freqs = jnp.exp(freq_steps * (-2.0 * math.log(ROPE_BASE) / rot_width))
    angles = positions.astype(jnp.float32)[:, None] * inv_freqs[None, :]
    angle_shape = (positions.shape[0],) + (1,) * (values.ndim - 2) + (half_width,)
    cosine = jnp.cos(angles).reshape(angle_shape)
    sine_part = jnp.sin(angles).reshape(angle_shape)
    lower_half = values[..., :half_width]
    upper_half = values[..., half_width:]
    return jnp.concatenate(
        [
            lower_half * cosine - upper_half * sine_part,
            upper_half * cosine + lower_half * sine_part,
        ],
        axis=-1,
    )


def queries_keys(projected, positions, latent_gain, up_heads):
    head_cols = H * (DN + DR)
    row_count = projected.shape[0]
    query_cols = projected[:, :head_cols].reshape(row_count, H, DN + DR)
    query_rot = rotate(query_cols[..., DN:].astype(jnp.float32), positions).astype(jnp.bfloat16)
    latent = rms_scale(projected[:, head_cols : head_cols + LAT], latent_gain).astype(jnp.bfloat16)
    key_rot = rotate(projected[:, head_cols + LAT :].astype(jnp.float32), positions).astype(
        jnp.bfloat16
    )
    query_lat = jnp.einsum(
        "rhn,lhn->rhl", query_cols[..., :DN], up_heads[..., :DN], preferred_element_type=jnp.float32
    ).astype(jnp.bfloat16)
    queries = jnp.concatenate([query_lat, query_rot], axis=-1)
    key_rows = jnp.concatenate([latent, key_rot], axis=-1)
    return (queries, key_rows)


def prompt_attention(queries, query_ids, all_keys, all_ids, score_scale):
    row_count = queries.shape[0]
    block_rows = min(row_count, 512)
    block_count = row_count // block_rows
    query_blocks = queries.reshape(block_count, block_rows, H, queries.shape[-1])
    id_blocks = query_ids.reshape(block_count, block_rows)
    latent_keys = all_keys[:, :LAT]

    def one_block(block_args):
        query_part, id_part = block_args
        scores = (
            jnp.einsum("qhc,kc->qhk", query_part, all_keys, preferred_element_type=jnp.float32)
            * score_scale
        )
        same_prompt = id_part[:, None] // LEN == all_ids[None, :] // LEN
        allowed = same_prompt & (all_ids[None, :] <= id_part[:, None])
        scores = jnp.where(allowed[:, None, :], scores, MASKED)
        peak_score = jnp.max(scores, axis=-1, keepdims=True)
        weights = jnp.where(allowed[:, None, :], jnp.exp(scores - peak_score), 0.0)
        weight_sum = jnp.sum(weights, axis=-1, keepdims=True)
        summed = jnp.einsum(
            "qhk,kl->qhl",
            weights.astype(jnp.bfloat16),
            latent_keys,
            preferred_element_type=jnp.float32,
        )
        return (summed / weight_sum).astype(jnp.bfloat16)

    return lax.map(one_block, (query_blocks, id_blocks)).reshape(row_count, H, LAT)


def page_attention(queries, own_score, latent_cache, page_table, cached_lengths, mp_index, score_scale):
    slot_count = latent_cache.shape[0]
    page_rows = latent_cache.shape[1]
    flat_cache = latent_cache.reshape(slot_count * page_rows, latent_cache.shape[2])
    slot_ids = mp_index * slot_count + jnp.arange(slot_count, dtype=jnp.int32)
    matches = page_table[:, :, None] == slot_ids[None, None, :]
    owned = jnp.any(matches, axis=1)
    page_numbers = jnp.arange(page_table.shape[1], dtype=jnp.int32)[None, :, None]
    page_index = jnp.sum(jnp.where(matches, page_numbers, 0), axis=1)
    key_position = (
        page_index[:, :, None] * page_rows + jnp.arange(page_rows, dtype=jnp.int32)[None, None, :]
    )
    allowed = owned[:, :, None] & (key_position < cached_lengths[:, None, None])
    allowed = allowed.reshape(page_table.shape[0], slot_count * page_rows)
    scores = (
        jnp.einsum("rhc,kc->rhk", queries, flat_cache, preferred_element_type=jnp.float32)
        * score_scale
    )
    scores = jnp.where(allowed[:, None, :], scores, MASKED)
    local_peak = jnp.max(scores, axis=-1)
    peak_score = jnp.maximum(lax.pmax(local_peak, "mp"), own_score)
    weights = jnp.where(allowed[:, None, :], jnp.exp(scores - peak_score[..., None]), 0.0)
    weight_sum = jnp.sum(weights, axis=-1)
    summed = jnp.einsum(
        "rhk,kl->rhl",
        weights.astype(jnp.bfloat16),
        flat_cache[:, :LAT],
        preferred_element_type=jnp.float32,
    )
    weight_sum, summed = lax.psum((weight_sum, summed), "mp")
    return (peak_score, weight_sum, summed)


def on_device(
    prompt_rows,
    step_rows,
    attn_gain,
    latent_gain,
    joined_qkva,
    kv_up,
    out_proj,
    latent_cache,
    page_table,
    cached_lengths,
):
    prompt_count = prompt_rows.shape[0]
    mp_index = lax.axis_index("mp")
    mp_size = lax.axis_size("mp")
    score_scale = (DN + DR) ** (-0.5)
    step_full = lax.all_gather(step_rows, "mp", axis=1, tiled=True)
    stacked = jnp.concatenate([prompt_rows, step_full], axis=0)
    normed = rms_scale(stacked, attn_gain).astype(jnp.bfloat16)
    prompt_ids = jnp.arange(prompt_count, dtype=jnp.int32)
    positions = jnp.concatenate([prompt_ids % LEN, cached_lengths], axis=0)
    served = tuple(gather_weight(w) for w in (joined_qkva, kv_up, out_proj))
    inputs = normed
    projected = jnp.dot(
        inputs,
        served[0],
        preferred_element_type=jnp.float32,
    )
    up_heads = served[1].reshape(LAT, H, DN + DV)
    queries, key_rows = queries_keys(
        projected.astype(jnp.bfloat16), positions, latent_gain, up_heads
    )
    prompt_queries = queries[:prompt_count]
    prompt_key_rows = key_rows[:prompt_count]
    step_queries = queries[prompt_count:]
    step_keys = key_rows[prompt_count:]
    prompt_latent = prompt_attention(
        prompt_queries, prompt_ids, prompt_key_rows, prompt_ids, score_scale
    )
    own_score = (
        jnp.einsum("rhc,rc->rh", step_queries, step_keys, preferred_element_type=jnp.float32)
        * score_scale
    )
    peak_score, weight_sum, summed = page_attention(
        step_queries, own_score, latent_cache, page_table, cached_lengths, mp_index, score_scale
    )
    own_weight = jnp.exp(own_score - peak_score)
    weight_sum = weight_sum + own_weight
    own_latent = step_keys[:, :LAT].astype(jnp.float32)
    own_half = own_weight.astype(jnp.bfloat16).astype(jnp.float32)
    summed = summed + own_half[..., None] * own_latent[:, None, :]
    step_latent = (summed / weight_sum[..., None]).astype(jnp.bfloat16)
    latent_out = jnp.concatenate([prompt_latent, step_latent], axis=0)
    heads_out = jnp.einsum(
        "rhl,lhv->rhv", latent_out, up_heads[..., DN:], preferred_element_type=jnp.float32
    ).astype(jnp.bfloat16)
    heads_out = heads_out.reshape(latent_out.shape[0], H * DV)
    inputs = heads_out
    attended = jnp.dot(
        inputs,
        served[2],
        preferred_element_type=jnp.float32,
    )
    attended = attended.astype(jnp.bfloat16)
    prompt_out = attended[:prompt_count]
    col_width = attended.shape[1] // mp_size
    step_out = lax.dynamic_slice_in_dim(attended[prompt_count:], mp_index * col_width, col_width, 1)
    return (prompt_out, step_out)


def solution(mesh):
    placed = (
        P(("dp", "mp"), None),
        P("dp", "mp"),
        P(),
        P(),
        P("dp", "mp"),
        P("dp", "mp"),
        P("dp", "mp"),
        P(("dp", "mp"), None, None),
        P("dp", None),
        P("dp"),
    )
    return jax.shard_map(
        on_device,
        mesh=mesh,
        in_specs=placed,
        out_specs=(P(("dp", "mp"), None), P("dp", "mp")),
        check_vma=False,
    )
```

```python
import math

import numpy as np

import jax
import jax.numpy as jnp
from jax import lax
from jax.sharding import PartitionSpec as P

H = 16
DN = 128
DR = 64
DV = 128
LAT = 512
LEN = 512


NORM_EPS = 1e-06
ROPE_BASE = 50000.0
MASKED = -1e30


AXES = ("dp", "mp")


def _coords(i):
    dp, mp = i // 32, i % 32
    return (2 * (dp // 2) + (mp // 4) % 2, mp % 4, mp // 8, dp % 2)


def _index(x, y, z, core):
    return ((x // 2) * 2 + core) * 32 + z * 8 + (x % 2) * 4 + y


def _shift_pairs(dim, step):
    pairs = []
    for i in range(128):
        c = list(_coords(i))
        c[dim] = (c[dim] + step) % 4
        pairs.append((i, _index(*c)))
    return pairs


def torus_gather(block, cuts):
    rows = block.shape[0]
    partner = lax.ppermute(block, "dp", [(d, d ^ 1) for d in range(4)])
    chip = jnp.concatenate([block, partner], axis=0)
    me = lax.axis_index(AXES)
    dp, mp = me // 32, me % 32
    cx, cy, cz, ccore = 2 * (dp // 2) + (mp // 4) % 2, mp % 4, mp // 8, dp % 2
    ids = np.arange(128)
    x = 2 * (ids // 64) + (ids % 32 // 4) % 2
    y = ids % 4
    z = ids % 32 // 8
    core = (ids // 32) % 2
    rel = ((x - cx) % 4) * 16 + ((y - cy) % 4) * 4 + (z - cz) % 4
    pieces = []
    for part in range(len(cuts) - 1):
        data = chip[:, cuts[part]:cuts[part + 1]]
        offs = [(0, 0, 0)]
        for stage in range(3):
            dim = (part + stage) % 3
            right = lax.ppermute(data, AXES, _shift_pairs(dim, 1))
            left = lax.ppermute(data, AXES, _shift_pairs(dim, -1))
            far = lax.ppermute(right, AXES, _shift_pairs(dim, 1))
            new_offs = list(offs)
            for delta in (-1, 1, -2):
                for o in offs:
                    o = list(o)
                    o[dim] = (o[dim] + delta) % 4
                    new_offs.append(tuple(o))
            data = jnp.concatenate([data, right, left, far], axis=0)
            offs = new_offs
        table = np.zeros((4, 4, 4), np.int32)
        for pos, o in enumerate(offs):
            table[o] = pos
        pick = jnp.take(jnp.asarray(table.reshape(-1)), rel, mode="clip") * 2 + (core - ccore) % 2
        slabs = data.reshape(-1, rows, data.shape[-1])
        pieces.append(jnp.take(slabs, pick, axis=0, mode="clip"))
    return jnp.concatenate(pieces, axis=2)


def gather_weights(joined, kv_up, out_proj):
    mp_size = 32
    j = joined.astype(jnp.bfloat16).reshape(mp_size, -1)
    k = kv_up.astype(jnp.bfloat16).reshape(mp_size, -1)
    o = out_proj.astype(jnp.bfloat16).reshape(mp_size, -1)
    packed = jnp.concatenate([j, k, o], axis=1)
    swapped = lax.all_to_all(packed, "mp", 0, 0, tiled=True)
    jw, kw = j.shape[1], k.shape[1]
    jr = swapped[:, :jw].reshape(mp_size, 16, 114).transpose(1, 0, 2).reshape(16, mp_size * 114)
    kr = swapped[:, jw:jw + kw].reshape(mp_size, 4, 128).transpose(1, 0, 2).reshape(16, 1024)
    orr = swapped[:, jw + kw:].reshape(mp_size, 16, 64).transpose(1, 0, 2).reshape(16, mp_size * 64)
    jr = jnp.pad(jr, ((0, 0), (0, 3712 - 3648)))
    block = jnp.concatenate([jr, orr, kr], axis=1)
    g = torus_gather(block, [0, 2304, 4608, 6784])
    w1 = g[:, :, :3648].reshape(2048, 3648)
    w3 = g[:, :, 3712:5760].reshape(2048, 2048)
    w2 = g[:, :, 5760:].reshape(128, 4, 4096).reshape(512, 4096)
    return w1, w2, w3


def rms_scale(values, scales):
    widened = values.astype(jnp.float32)
    mean_square = jnp.mean(widened * widened, axis=-1, keepdims=True)
    return widened * lax.rsqrt(mean_square + NORM_EPS) * scales


def rotate(values, positions):
    rot_width = values.shape[-1]
    half_width = rot_width // 2
    freq_steps = jnp.arange(half_width, dtype=jnp.float32)
    inv_freqs = jnp.exp(freq_steps * (-2.0 * math.log(ROPE_BASE) / rot_width))
    angles = positions.astype(jnp.float32)[:, None] * inv_freqs[None, :]
    angle_shape = (positions.shape[0],) + (1,) * (values.ndim - 2) + (half_width,)
    cosine = jnp.cos(angles).reshape(angle_shape)
    sine_part = jnp.sin(angles).reshape(angle_shape)
    lower_half = values[..., :half_width]
    upper_half = values[..., half_width:]
    return jnp.concatenate(
        [
            lower_half * cosine - upper_half * sine_part,
            upper_half * cosine + lower_half * sine_part,
        ],
        axis=-1,
    )


def queries_keys(projected, positions, latent_gain, up_heads):
    head_cols = H * (DN + DR)
    row_count = projected.shape[0]
    query_cols = projected[:, :head_cols].reshape(row_count, H, DN + DR)
    query_rot = rotate(query_cols[..., DN:].astype(jnp.float32), positions).astype(jnp.bfloat16)
    latent = rms_scale(projected[:, head_cols : head_cols + LAT], latent_gain).astype(jnp.bfloat16)
    key_rot = rotate(projected[:, head_cols + LAT :].astype(jnp.float32), positions).astype(
        jnp.bfloat16
    )
    query_lat = jnp.einsum(
        "rhn,lhn->rhl", query_cols[..., :DN], up_heads[..., :DN], preferred_element_type=jnp.float32
    ).astype(jnp.bfloat16)
    queries = jnp.concatenate([query_lat, query_rot], axis=-1)
    key_rows = jnp.concatenate([latent, key_rot], axis=-1)
    return (queries, key_rows)


def prompt_attention(queries, query_ids, all_keys, all_ids, score_scale):
    row_count = queries.shape[0]
    block_rows = min(row_count, 512)
    block_count = row_count // block_rows
    query_blocks = queries.reshape(block_count, block_rows, H, queries.shape[-1])
    id_blocks = query_ids.reshape(block_count, block_rows)
    latent_keys = all_keys[:, :LAT]

    def one_block(block_args):
        query_part, id_part = block_args
        scores = (
            jnp.einsum("qhc,kc->qhk", query_part, all_keys, preferred_element_type=jnp.float32)
            * score_scale
        )
        same_prompt = id_part[:, None] // LEN == all_ids[None, :] // LEN
        allowed = same_prompt & (all_ids[None, :] <= id_part[:, None])
        scores = jnp.where(allowed[:, None, :], scores, MASKED)
        peak_score = jnp.max(scores, axis=-1, keepdims=True)
        weights = jnp.where(allowed[:, None, :], jnp.exp(scores - peak_score), 0.0)
        weight_sum = jnp.sum(weights, axis=-1, keepdims=True)
        summed = jnp.einsum(
            "qhk,kl->qhl",
            weights.astype(jnp.bfloat16),
            latent_keys,
            preferred_element_type=jnp.float32,
        )
        return (summed / weight_sum).astype(jnp.bfloat16)

    return lax.map(one_block, (query_blocks, id_blocks)).reshape(row_count, H, LAT)


def step_attention(queries, own_keys, latent_cache, page_table, cached_lengths, score_scale):
    pool = lax.all_gather(latent_cache, "mp", axis=0, tiled=True)
    request_count, page_count = page_table.shape
    page_rows = pool.shape[1]
    pages = pool[page_table].reshape(request_count, page_count * page_rows, pool.shape[2])
    key_all = jnp.concatenate([pages, own_keys[:, None, :]], axis=1)
    cached_ok = (
        jnp.arange(page_count * page_rows, dtype=jnp.int32)[None, :] < cached_lengths[:, None]
    )
    allowed = jnp.concatenate([cached_ok, jnp.ones((request_count, 1), jnp.bool_)], axis=1)
    scores = (
        jnp.einsum("rhc,rkc->rhk", queries, key_all, preferred_element_type=jnp.float32)
        * score_scale
    )
    scores = jnp.where(allowed[:, None, :], scores, MASKED)
    peak_score = jnp.max(scores, axis=-1, keepdims=True)
    weights = jnp.where(allowed[:, None, :], jnp.exp(scores - peak_score), 0.0)
    weight_sum = jnp.sum(weights, axis=-1, keepdims=True)
    summed = jnp.einsum(
        "rhk,rkl->rhl",
        weights.astype(jnp.bfloat16),
        key_all[:, :, :LAT],
        preferred_element_type=jnp.float32,
    )
    return (summed / weight_sum).astype(jnp.bfloat16)


def on_device(
    prompt_rows,
    step_rows,
    attn_gain,
    latent_gain,
    joined_qkva,
    kv_up,
    out_proj,
    latent_cache,
    page_table,
    cached_lengths,
):
    prompt_count = prompt_rows.shape[0]
    mp_index = lax.axis_index("mp")
    mp_size = lax.axis_size("mp")
    score_scale = (DN + DR) ** (-0.5)
    step_full = lax.all_gather(step_rows, "mp", axis=1, tiled=True)
    stacked = jnp.concatenate([prompt_rows, step_full], axis=0)
    normed = rms_scale(stacked, attn_gain).astype(jnp.bfloat16)
    prompt_ids = jnp.arange(prompt_count, dtype=jnp.int32)
    positions = jnp.concatenate([prompt_ids % LEN, cached_lengths], axis=0)
    served = gather_weights(joined_qkva, kv_up, out_proj)
    inputs = normed
    projected = jnp.dot(
        inputs,
        served[0],
        preferred_element_type=jnp.float32,
    )
    up_heads = served[1].reshape(LAT, H, DN + DV)
    queries, key_rows = queries_keys(
        projected.astype(jnp.bfloat16), positions, latent_gain, up_heads
    )
    prompt_queries = queries[:prompt_count]
    prompt_key_rows = key_rows[:prompt_count]
    step_queries = queries[prompt_count:]
    step_keys = key_rows[prompt_count:]
    prompt_latent = prompt_attention(
        prompt_queries, prompt_ids, prompt_key_rows, prompt_ids, score_scale
    )
    step_latent = step_attention(
        step_queries, step_keys, latent_cache, page_table, cached_lengths, score_scale
    )
    latent_out = jnp.concatenate([prompt_latent, step_latent], axis=0)
    heads_out = jnp.einsum(
        "rhl,lhv->rhv", latent_out, up_heads[..., DN:], preferred_element_type=jnp.float32
    ).astype(jnp.bfloat16)
    heads_out = heads_out.reshape(latent_out.shape[0], H * DV)
    inputs = heads_out
    attended = jnp.dot(
        inputs,
        served[2],
        preferred_element_type=jnp.float32,
    )
    attended = attended.astype(jnp.bfloat16)
    prompt_out = attended[:prompt_count]
    col_width = attended.shape[1] // mp_size
    step_out = lax.dynamic_slice_in_dim(attended[prompt_count:], mp_index * col_width, col_width, 1)
    return (prompt_out, step_out)


def solution(mesh):
    placed = (
        P(("dp", "mp"), None),
        P("dp", "mp"),
        P(),
        P(),
        P("dp", "mp"),
        P("dp", "mp"),
        P("dp", "mp"),
        P(("dp", "mp"), None, None),
        P("dp", None),
        P("dp"),
    )
    return jax.shard_map(
        on_device,
        mesh=mesh,
        in_specs=placed,
        out_specs=(P(("dp", "mp"), None), P("dp", "mp")),
        check_vma=False,
    )
```

```python
import math

import numpy as np

import jax
import jax.numpy as jnp
from jax import lax
from jax.sharding import PartitionSpec as P

H = 16
DN = 128
DR = 64
DV = 128
LAT = 512
LEN = 512


NORM_EPS = 1e-06
ROPE_BASE = 50000.0
MASKED = -1e30


AXES = ("dp", "mp")


def _coords(i):
    dp, mp = i // 32, i % 32
    return (2 * (dp // 2) + (mp // 4) % 2, mp % 4, mp // 8, dp % 2)


def _index(x, y, z, core):
    return ((x // 2) * 2 + core) * 32 + z * 8 + (x % 2) * 4 + y


def _shift_pairs(dim, step):
    pairs = []
    for i in range(128):
        c = list(_coords(i))
        c[dim] = (c[dim] + step) % 4
        pairs.append((i, _index(*c)))
    return pairs


def torus_gather(block, cuts):
    rows = block.shape[0]
    partner = lax.ppermute(block, "dp", [(d, d ^ 1) for d in range(4)])
    chip = jnp.concatenate([block, partner], axis=0)
    me = lax.axis_index(AXES)
    dp, mp = me // 32, me % 32
    cx, cy, cz, ccore = 2 * (dp // 2) + (mp // 4) % 2, mp % 4, mp // 8, dp % 2
    ids = np.arange(128)
    x = 2 * (ids // 64) + (ids % 32 // 4) % 2
    y = ids % 4
    z = ids % 32 // 8
    core = (ids // 32) % 2
    rel = ((x - cx) % 4) * 16 + ((y - cy) % 4) * 4 + (z - cz) % 4
    pieces = []
    for part in range(len(cuts) - 1):
        data = chip[:, cuts[part]:cuts[part + 1]]
        offs = [(0, 0, 0)]
        for stage in range(3):
            dim = (part + stage) % 3
            right = lax.ppermute(data, AXES, _shift_pairs(dim, 1))
            left = lax.ppermute(data, AXES, _shift_pairs(dim, -1))
            far = lax.ppermute(right, AXES, _shift_pairs(dim, 1))
            new_offs = list(offs)
            for delta in (-1, 1, -2):
                for o in offs:
                    o = list(o)
                    o[dim] = (o[dim] + delta) % 4
                    new_offs.append(tuple(o))
            data = jnp.concatenate([data, right, left, far], axis=0)
            offs = new_offs
        table = np.zeros((4, 4, 4), np.int32)
        for pos, o in enumerate(offs):
            table[o] = pos
        pick = jnp.take(jnp.asarray(table.reshape(-1)), rel, mode="clip") * 2 + (core - ccore) % 2
        slabs = data.reshape(-1, rows, data.shape[-1])
        pieces.append(jnp.take(slabs, pick, axis=0, mode="clip"))
    return jnp.concatenate(pieces, axis=2)


def gather_weights(joined, kv_up, out_proj, step_rows):
    mp_size = 32
    j = joined.astype(jnp.bfloat16).reshape(mp_size, -1)
    k = kv_up.astype(jnp.bfloat16).reshape(mp_size, -1)
    o = out_proj.astype(jnp.bfloat16).reshape(mp_size, -1)
    packed = jnp.concatenate([j, k, o], axis=1)
    swapped = lax.all_to_all(packed, "mp", 0, 0, tiled=True)
    jw, kw = j.shape[1], k.shape[1]
    jr = swapped[:, :jw].reshape(mp_size, 16, 114).transpose(1, 0, 2).reshape(16, mp_size * 114)
    kr = swapped[:, jw:jw + kw].reshape(mp_size, 4, 128).transpose(1, 0, 2).reshape(16, 1024)
    orr = swapped[:, jw + kw:].reshape(mp_size, 16, 64).transpose(1, 0, 2).reshape(16, mp_size * 64)
    jr = jnp.pad(jr, ((0, 0), (0, 3712 - 3648)))
    step_count, step_width = step_rows.shape
    step_block = jnp.pad(step_rows, ((0, 16 - step_count), (0, 128 - step_width)))
    block = jnp.concatenate([jr, orr, kr, step_block], axis=1)
    g = torus_gather(block, [0, 2304, 4608, 6912])
    w1 = g[:, :, :3648].reshape(2048, 3648)
    w3 = g[:, :, 3712:5760].reshape(2048, 2048)
    w2 = g[:, :, 5760:6784].reshape(128, 4, 4096).reshape(512, 4096)
    steps = lax.dynamic_slice_in_dim(g[:, :step_count, 6784:6784 + step_width], lax.axis_index("dp") * mp_size, mp_size, 0)
    steps = steps.transpose(1, 0, 2).reshape(step_count, mp_size * step_width)
    return w1, w2, w3, steps


def rms_scale(values, scales):
    widened = values.astype(jnp.float32)
    mean_square = jnp.mean(widened * widened, axis=-1, keepdims=True)
    return widened * lax.rsqrt(mean_square + NORM_EPS) * scales


def rotate(values, positions):
    rot_width = values.shape[-1]
    half_width = rot_width // 2
    freq_steps = jnp.arange(half_width, dtype=jnp.float32)
    inv_freqs = jnp.exp(freq_steps * (-2.0 * math.log(ROPE_BASE) / rot_width))
    angles = positions.astype(jnp.float32)[:, None] * inv_freqs[None, :]
    angle_shape = (positions.shape[0],) + (1,) * (values.ndim - 2) + (half_width,)
    cosine = jnp.cos(angles).reshape(angle_shape)
    sine_part = jnp.sin(angles).reshape(angle_shape)
    lower_half = values[..., :half_width]
    upper_half = values[..., half_width:]
    return jnp.concatenate(
        [
            lower_half * cosine - upper_half * sine_part,
            upper_half * cosine + lower_half * sine_part,
        ],
        axis=-1,
    )


def queries_keys(projected, positions, latent_gain, up_heads):
    head_cols = H * (DN + DR)
    row_count = projected.shape[0]
    query_cols = projected[:, :head_cols].reshape(row_count, H, DN + DR)
    query_rot = rotate(query_cols[..., DN:].astype(jnp.float32), positions).astype(jnp.bfloat16)
    latent = rms_scale(projected[:, head_cols : head_cols + LAT], latent_gain).astype(jnp.bfloat16)
    key_rot = rotate(projected[:, head_cols + LAT :].astype(jnp.float32), positions).astype(
        jnp.bfloat16
    )
    query_lat = jnp.einsum(
        "rhn,lhn->rhl", query_cols[..., :DN], up_heads[..., :DN], preferred_element_type=jnp.float32
    ).astype(jnp.bfloat16)
    queries = jnp.concatenate([query_lat, query_rot], axis=-1)
    key_rows = jnp.concatenate([latent, key_rot], axis=-1)
    return (queries, key_rows)


def prompt_attention(queries, query_ids, all_keys, all_ids, score_scale):
    row_count = queries.shape[0]
    block_rows = min(row_count, 512)
    block_count = row_count // block_rows
    query_blocks = queries.reshape(block_count, block_rows, H, queries.shape[-1])
    id_blocks = query_ids.reshape(block_count, block_rows)
    latent_keys = all_keys[:, :LAT]

    def one_block(block_args):
        query_part, id_part = block_args
        scores = (
            jnp.einsum("qhc,kc->qhk", query_part, all_keys, preferred_element_type=jnp.float32)
            * score_scale
        )
        same_prompt = id_part[:, None] // LEN == all_ids[None, :] // LEN
        allowed = same_prompt & (all_ids[None, :] <= id_part[:, None])
        scores = jnp.where(allowed[:, None, :], scores, MASKED)
        peak_score = jnp.max(scores, axis=-1, keepdims=True)
        weights = jnp.where(allowed[:, None, :], jnp.exp(scores - peak_score), 0.0)
        weight_sum = jnp.sum(weights, axis=-1, keepdims=True)
        summed = jnp.einsum(
            "qhk,kl->qhl",
            weights.astype(jnp.bfloat16),
            latent_keys,
            preferred_element_type=jnp.float32,
        )
        return (summed / weight_sum).astype(jnp.bfloat16)

    return lax.map(one_block, (query_blocks, id_blocks)).reshape(row_count, H, LAT)


def step_attention(queries, own_keys, latent_cache, page_table, cached_lengths, score_scale):
    pool = lax.all_gather(latent_cache, "mp", axis=0, tiled=True)
    request_count, page_count = page_table.shape
    page_rows = pool.shape[1]
    pages = pool[page_table].reshape(request_count, page_count * page_rows, pool.shape[2])
    key_all = jnp.concatenate([pages, own_keys[:, None, :]], axis=1)
    cached_ok = (
        jnp.arange(page_count * page_rows, dtype=jnp.int32)[None, :] < cached_lengths[:, None]
    )
    allowed = jnp.concatenate([cached_ok, jnp.ones((request_count, 1), jnp.bool_)], axis=1)
    scores = (
        jnp.einsum("rhc,rkc->rhk", queries, key_all, preferred_element_type=jnp.float32)
        * score_scale
    )
    scores = jnp.where(allowed[:, None, :], scores, MASKED)
    peak_score = jnp.max(scores, axis=-1, keepdims=True)
    weights = jnp.where(allowed[:, None, :], jnp.exp(scores - peak_score), 0.0)
    weight_sum = jnp.sum(weights, axis=-1, keepdims=True)
    summed = jnp.einsum(
        "rhk,rkl->rhl",
        weights.astype(jnp.bfloat16),
        key_all[:, :, :LAT],
        preferred_element_type=jnp.float32,
    )
    return (summed / weight_sum).astype(jnp.bfloat16)


def on_device(
    prompt_rows,
    step_rows,
    attn_gain,
    latent_gain,
    joined_qkva,
    kv_up,
    out_proj,
    latent_cache,
    page_table,
    cached_lengths,
):
    prompt_count = prompt_rows.shape[0]
    mp_index = lax.axis_index("mp")
    mp_size = lax.axis_size("mp")
    score_scale = (DN + DR) ** (-0.5)
    *served, step_full = gather_weights(joined_qkva, kv_up, out_proj, step_rows)
    stacked = jnp.concatenate([prompt_rows, step_full], axis=0)
    normed = rms_scale(stacked, attn_gain).astype(jnp.bfloat16)
    prompt_ids = jnp.arange(prompt_count, dtype=jnp.int32)
    positions = jnp.concatenate([prompt_ids % LEN, cached_lengths], axis=0)
    inputs = normed
    projected = jnp.dot(
        inputs,
        served[0],
        preferred_element_type=jnp.float32,
    )
    up_heads = served[1].reshape(LAT, H, DN + DV)
    queries, key_rows = queries_keys(
        projected.astype(jnp.bfloat16), positions, latent_gain, up_heads
    )
    prompt_queries = queries[:prompt_count]
    prompt_key_rows = key_rows[:prompt_count]
    step_queries = queries[prompt_count:]
    step_keys = key_rows[prompt_count:]
    prompt_latent = prompt_attention(
        prompt_queries, prompt_ids, prompt_key_rows, prompt_ids, score_scale
    )
    step_latent = step_attention(
        step_queries, step_keys, latent_cache, page_table, cached_lengths, score_scale
    )
    latent_out = jnp.concatenate([prompt_latent, step_latent], axis=0)
    heads_out = jnp.einsum(
        "rhl,lhv->rhv", latent_out, up_heads[..., DN:], preferred_element_type=jnp.float32
    ).astype(jnp.bfloat16)
    heads_out = heads_out.reshape(latent_out.shape[0], H * DV)
    inputs = heads_out
    attended = jnp.dot(
        inputs,
        served[2],
        preferred_element_type=jnp.float32,
    )
    attended = attended.astype(jnp.bfloat16)
    prompt_out = attended[:prompt_count]
    col_width = attended.shape[1] // mp_size
    step_out = lax.dynamic_slice_in_dim(attended[prompt_count:], mp_index * col_width, col_width, 1)
    return (prompt_out, step_out)


def solution(mesh):
    placed = (
        P(("dp", "mp"), None),
        P("dp", "mp"),
        P(),
        P(),
        P("dp", "mp"),
        P("dp", "mp"),
        P("dp", "mp"),
        P(("dp", "mp"), None, None),
        P("dp", None),
        P("dp"),
    )
    return jax.shard_map(
        on_device,
        mesh=mesh,
        in_specs=placed,
        out_specs=(P(("dp", "mp"), None), P("dp", "mp")),
        check_vma=False,
    )
```

```python
import math

import numpy as np

import jax
import jax.numpy as jnp
from jax import lax
from jax.sharding import PartitionSpec as P

H = 16
DN = 128
DR = 64
DV = 128
LAT = 512
LEN = 512


NORM_EPS = 1e-06
ROPE_BASE = 50000.0
MASKED = -1e30


AXES = ("dp", "mp")


def _coords(i):
    dp, mp = i // 32, i % 32
    return (2 * (dp // 2) + (mp // 4) % 2, mp % 4, mp // 8, dp % 2)


def _index(x, y, z, core):
    return ((x // 2) * 2 + core) * 32 + z * 8 + (x % 2) * 4 + y


def _shift_pairs(dim, step):
    pairs = []
    for i in range(128):
        c = list(_coords(i))
        c[dim] = (c[dim] + step) % 4
        pairs.append((i, _index(*c)))
    return pairs


def torus_gather(block, cuts):
    rows = block.shape[0]
    partner = lax.ppermute(block, "dp", [(d, d ^ 1) for d in range(4)])
    chip = jnp.concatenate([block, partner], axis=0)
    me = lax.axis_index(AXES)
    dp, mp = me // 32, me % 32
    cx, cy, cz, ccore = 2 * (dp // 2) + (mp // 4) % 2, mp % 4, mp // 8, dp % 2
    ids = np.arange(128)
    x = 2 * (ids // 64) + (ids % 32 // 4) % 2
    y = ids % 4
    z = ids % 32 // 8
    core = (ids // 32) % 2
    rel = ((x - cx) % 4) * 16 + ((y - cy) % 4) * 4 + (z - cz) % 4
    pieces = []
    for part in range(len(cuts) - 1):
        data = chip[:, cuts[part]:cuts[part + 1]]
        offs = [(0, 0, 0)]
        for stage in range(3):
            dim = (part + stage) % 3
            right = lax.ppermute(data, AXES, _shift_pairs(dim, 1))
            left = lax.ppermute(data, AXES, _shift_pairs(dim, -1))
            half = data.shape[0] // 2
            far = jnp.concatenate(
                [
                    lax.ppermute(right[:half], AXES, _shift_pairs(dim, 1)),
                    lax.ppermute(left[half:], AXES, _shift_pairs(dim, -1)),
                ],
                axis=0,
            )
            new_offs = list(offs)
            for delta in (-1, 1, -2):
                for o in offs:
                    o = list(o)
                    o[dim] = (o[dim] + delta) % 4
                    new_offs.append(tuple(o))
            data = jnp.concatenate([data, right, left, far], axis=0)
            offs = new_offs
        table = np.zeros((4, 4, 4), np.int32)
        for pos, o in enumerate(offs):
            table[o] = pos
        pick = jnp.take(jnp.asarray(table.reshape(-1)), rel, mode="clip") * 2 + (core - ccore) % 2
        slabs = data.reshape(-1, rows, data.shape[-1])
        pieces.append(jnp.take(slabs, pick, axis=0, mode="clip"))
    return jnp.concatenate(pieces, axis=2)


def gather_weights(joined, kv_up, out_proj, step_rows):
    mp_size = 32
    j = joined.astype(jnp.bfloat16).reshape(mp_size, -1)
    k = kv_up.astype(jnp.bfloat16).reshape(mp_size, -1)
    o = out_proj.astype(jnp.bfloat16).reshape(mp_size, -1)
    packed = jnp.concatenate([j, k, o], axis=1)
    swapped = lax.all_to_all(packed, "mp", 0, 0, tiled=True)
    jw, kw = j.shape[1], k.shape[1]
    jr = swapped[:, :jw].reshape(mp_size, 16, 114).transpose(1, 0, 2).reshape(16, mp_size * 114)
    kr = swapped[:, jw:jw + kw].reshape(mp_size, 4, 128).transpose(1, 0, 2).reshape(16, 1024)
    orr = swapped[:, jw + kw:].reshape(mp_size, 16, 64).transpose(1, 0, 2).reshape(16, mp_size * 64)
    jr = jnp.pad(jr, ((0, 0), (0, 3712 - 3648)))
    step_count, step_width = step_rows.shape
    step_block = jnp.pad(step_rows, ((0, 16 - step_count), (0, 128 - step_width)))
    block = jnp.concatenate([jr, orr, kr, step_block], axis=1)
    g = torus_gather(block, [0, 2304, 4608, 6912])
    w1 = g[:, :, :3648].reshape(2048, 3648)
    w3 = g[:, :, 3712:5760].reshape(2048, 2048)
    w2 = g[:, :, 5760:6784].reshape(128, 4, 4096).reshape(512, 4096)
    steps = lax.dynamic_slice_in_dim(g[:, :step_count, 6784:6784 + step_width], lax.axis_index("dp") * mp_size, mp_size, 0)
    steps = steps.transpose(1, 0, 2).reshape(step_count, mp_size * step_width)
    return w1, w2, w3, steps


def rms_scale(values, scales):
    widened = values.astype(jnp.float32)
    mean_square = jnp.mean(widened * widened, axis=-1, keepdims=True)
    return widened * lax.rsqrt(mean_square + NORM_EPS) * scales


def rotate(values, positions):
    rot_width = values.shape[-1]
    half_width = rot_width // 2
    freq_steps = jnp.arange(half_width, dtype=jnp.float32)
    inv_freqs = jnp.exp(freq_steps * (-2.0 * math.log(ROPE_BASE) / rot_width))
    angles = positions.astype(jnp.float32)[:, None] * inv_freqs[None, :]
    angle_shape = (positions.shape[0],) + (1,) * (values.ndim - 2) + (half_width,)
    cosine = jnp.cos(angles).reshape(angle_shape)
    sine_part = jnp.sin(angles).reshape(angle_shape)
    lower_half = values[..., :half_width]
    upper_half = values[..., half_width:]
    return jnp.concatenate(
        [
            lower_half * cosine - upper_half * sine_part,
            upper_half * cosine + lower_half * sine_part,
        ],
        axis=-1,
    )


def queries_keys(projected, positions, latent_gain, up_heads):
    head_cols = H * (DN + DR)
    row_count = projected.shape[0]
    query_cols = projected[:, :head_cols].reshape(row_count, H, DN + DR)
    query_rot = rotate(query_cols[..., DN:].astype(jnp.float32), positions).astype(jnp.bfloat16)
    latent = rms_scale(projected[:, head_cols : head_cols + LAT], latent_gain).astype(jnp.bfloat16)
    key_rot = rotate(projected[:, head_cols + LAT :].astype(jnp.float32), positions).astype(
        jnp.bfloat16
    )
    query_lat = jnp.einsum(
        "rhn,lhn->rhl", query_cols[..., :DN], up_heads[..., :DN], preferred_element_type=jnp.float32
    ).astype(jnp.bfloat16)
    queries = jnp.concatenate([query_lat, query_rot], axis=-1)
    key_rows = jnp.concatenate([latent, key_rot], axis=-1)
    return (queries, key_rows)


def prompt_attention(queries, query_ids, all_keys, all_ids, score_scale):
    row_count = queries.shape[0]
    block_rows = min(row_count, 512)
    block_count = row_count // block_rows
    query_blocks = queries.reshape(block_count, block_rows, H, queries.shape[-1])
    id_blocks = query_ids.reshape(block_count, block_rows)
    latent_keys = all_keys[:, :LAT]

    def one_block(block_args):
        query_part, id_part = block_args
        scores = (
            jnp.einsum("qhc,kc->qhk", query_part, all_keys, preferred_element_type=jnp.float32)
            * score_scale
        )
        same_prompt = id_part[:, None] // LEN == all_ids[None, :] // LEN
        allowed = same_prompt & (all_ids[None, :] <= id_part[:, None])
        scores = jnp.where(allowed[:, None, :], scores, MASKED)
        peak_score = jnp.max(scores, axis=-1, keepdims=True)
        weights = jnp.where(allowed[:, None, :], jnp.exp(scores - peak_score), 0.0)
        weight_sum = jnp.sum(weights, axis=-1, keepdims=True)
        summed = jnp.einsum(
            "qhk,kl->qhl",
            weights.astype(jnp.bfloat16),
            latent_keys,
            preferred_element_type=jnp.float32,
        )
        return (summed / weight_sum).astype(jnp.bfloat16)

    return lax.map(one_block, (query_blocks, id_blocks)).reshape(row_count, H, LAT)


def step_attention(queries, own_keys, latent_cache, page_table, cached_lengths, score_scale):
    pool = lax.all_gather(latent_cache, "mp", axis=0, tiled=True)
    request_count, page_count = page_table.shape
    page_rows = pool.shape[1]
    pages = pool[page_table].reshape(request_count, page_count * page_rows, pool.shape[2])
    key_all = jnp.concatenate([pages, own_keys[:, None, :]], axis=1)
    cached_ok = (
        jnp.arange(page_count * page_rows, dtype=jnp.int32)[None, :] < cached_lengths[:, None]
    )
    allowed = jnp.concatenate([cached_ok, jnp.ones((request_count, 1), jnp.bool_)], axis=1)
    scores = (
        jnp.einsum("rhc,rkc->rhk", queries, key_all, preferred_element_type=jnp.float32)
        * score_scale
    )
    scores = jnp.where(allowed[:, None, :], scores, MASKED)
    peak_score = jnp.max(scores, axis=-1, keepdims=True)
    weights = jnp.where(allowed[:, None, :], jnp.exp(scores - peak_score), 0.0)
    weight_sum = jnp.sum(weights, axis=-1, keepdims=True)
    summed = jnp.einsum(
        "rhk,rkl->rhl",
        weights.astype(jnp.bfloat16),
        key_all[:, :, :LAT],
        preferred_element_type=jnp.float32,
    )
    return (summed / weight_sum).astype(jnp.bfloat16)


def on_device(
    prompt_rows,
    step_rows,
    attn_gain,
    latent_gain,
    joined_qkva,
    kv_up,
    out_proj,
    latent_cache,
    page_table,
    cached_lengths,
):
    prompt_count = prompt_rows.shape[0]
    mp_index = lax.axis_index("mp")
    mp_size = lax.axis_size("mp")
    score_scale = (DN + DR) ** (-0.5)
    *served, step_full = gather_weights(joined_qkva, kv_up, out_proj, step_rows)
    stacked = jnp.concatenate([prompt_rows, step_full], axis=0)
    normed = rms_scale(stacked, attn_gain).astype(jnp.bfloat16)
    prompt_ids = jnp.arange(prompt_count, dtype=jnp.int32)
    positions = jnp.concatenate([prompt_ids % LEN, cached_lengths], axis=0)
    inputs = normed
    projected = jnp.dot(
        inputs,
        served[0],
        preferred_element_type=jnp.float32,
    )
    up_heads = served[1].reshape(LAT, H, DN + DV)
    queries, key_rows = queries_keys(
        projected.astype(jnp.bfloat16), positions, latent_gain, up_heads
    )
    prompt_queries = queries[:prompt_count]
    prompt_key_rows = key_rows[:prompt_count]
    step_queries = queries[prompt_count:]
    step_keys = key_rows[prompt_count:]
    prompt_latent = prompt_attention(
        prompt_queries, prompt_ids, prompt_key_rows, prompt_ids, score_scale
    )
    step_latent = step_attention(
        step_queries, step_keys, latent_cache, page_table, cached_lengths, score_scale
    )
    latent_out = jnp.concatenate([prompt_latent, step_latent], axis=0)
    heads_out = jnp.einsum(
        "rhl,lhv->rhv", latent_out, up_heads[..., DN:], preferred_element_type=jnp.float32
    ).astype(jnp.bfloat16)
    heads_out = heads_out.reshape(latent_out.shape[0], H * DV)
    inputs = heads_out
    attended = jnp.dot(
        inputs,
        served[2],
        preferred_element_type=jnp.float32,
    )
    attended = attended.astype(jnp.bfloat16)
    prompt_out = attended[:prompt_count]
    col_width = attended.shape[1] // mp_size
    step_out = lax.dynamic_slice_in_dim(attended[prompt_count:], mp_index * col_width, col_width, 1)
    return (prompt_out, step_out)


def solution(mesh):
    placed = (
        P(("dp", "mp"), None),
        P("dp", "mp"),
        P(),
        P(),
        P("dp", "mp"),
        P("dp", "mp"),
        P("dp", "mp"),
        P(("dp", "mp"), None, None),
        P("dp", None),
        P("dp"),
    )
    return jax.shard_map(
        on_device,
        mesh=mesh,
        in_specs=placed,
        out_specs=(P(("dp", "mp"), None), P("dp", "mp")),
        check_vma=False,
    )
```

```python
import math

import numpy as np

import jax
import jax.numpy as jnp
from jax import lax
from jax.sharding import PartitionSpec as P

H = 16
DN = 128
DR = 64
DV = 128
LAT = 512
LEN = 512


NORM_EPS = 1e-06
ROPE_BASE = 50000.0
MASKED = -1e30


AXES = ("dp", "mp")


def _coords(i):
    dp, mp = i // 32, i % 32
    return (2 * (dp // 2) + (mp // 4) % 2, mp % 4, mp // 8, dp % 2)


def _index(x, y, z, core):
    return ((x // 2) * 2 + core) * 32 + z * 8 + (x % 2) * 4 + y


def _shift_pairs(dim, step):
    pairs = []
    for i in range(128):
        c = list(_coords(i))
        c[dim] = (c[dim] + step) % 4
        pairs.append((i, _index(*c)))
    return pairs


def torus_gather(block, cuts):
    rows = block.shape[0]
    partner = lax.ppermute(block, "dp", [(d, d ^ 1) for d in range(4)])
    chip = jnp.concatenate([block, partner], axis=0)
    me = lax.axis_index(AXES)
    dp, mp = me // 32, me % 32
    cx, cy, cz, ccore = 2 * (dp // 2) + (mp // 4) % 2, mp % 4, mp // 8, dp % 2
    ids = np.arange(128)
    x = 2 * (ids // 64) + (ids % 32 // 4) % 2
    y = ids % 4
    z = ids % 32 // 8
    core = (ids // 32) % 2
    rel = ((x - cx) % 4) * 16 + ((y - cy) % 4) * 4 + (z - cz) % 4
    pieces = []
    for part in range(len(cuts) - 1):
        data = chip[:, cuts[part]:cuts[part + 1]]
        offs = [(0, 0, 0)]
        for stage in range(3):
            dim = (part + stage) % 3
            right = lax.ppermute(data, AXES, _shift_pairs(dim, 1))
            left = lax.ppermute(data, AXES, _shift_pairs(dim, -1))
            far = lax.ppermute(right, AXES, _shift_pairs(dim, 1))
            new_offs = list(offs)
            for delta in (-1, 1, -2):
                for o in offs:
                    o = list(o)
                    o[dim] = (o[dim] + delta) % 4
                    new_offs.append(tuple(o))
            data = jnp.concatenate([data, right, left, far], axis=0)
            offs = new_offs
        table = np.zeros((4, 4, 4), np.int32)
        for pos, o in enumerate(offs):
            table[o] = pos
        pick = jnp.take(jnp.asarray(table.reshape(-1)), rel, mode="clip") * 2 + (core - ccore) % 2
        slabs = data.reshape(-1, rows, data.shape[-1])
        pieces.append(jnp.take(slabs, pick, axis=0, mode="clip"))
    return jnp.concatenate(pieces, axis=2)


def gather_weights(joined, kv_up, out_proj, step_rows):
    mp_size = 32
    j = joined.astype(jnp.bfloat16).reshape(mp_size, -1)
    k = kv_up.astype(jnp.bfloat16).reshape(mp_size, -1)
    o = out_proj.astype(jnp.bfloat16).reshape(mp_size, -1)
    packed = jnp.concatenate([j, k, o], axis=1)
    swapped = lax.all_to_all(packed, "mp", 0, 0, tiled=True)
    jw, kw = j.shape[1], k.shape[1]
    jr = swapped[:, :jw].reshape(mp_size, 16, 114).transpose(1, 0, 2).reshape(16, mp_size * 114)
    kr = swapped[:, jw:jw + kw].reshape(mp_size, 4, 128).transpose(1, 0, 2).reshape(16, 1024)
    orr = swapped[:, jw + kw:].reshape(mp_size, 16, 64).transpose(1, 0, 2).reshape(16, mp_size * 64)
    jr = jnp.pad(jr, ((0, 0), (0, 3712 - 3648)))
    step_count, step_width = step_rows.shape
    step_block = jnp.pad(step_rows, ((0, 16 - step_count), (0, 128 - step_width)))
    block = jnp.concatenate([jr, orr, kr, step_block], axis=1)
    g = torus_gather(block, [0, 2304, 4608, 6912])
    w1 = g[:, :, :3648].reshape(2048, 3648)
    w3 = g[:, :, 3712:5760].reshape(2048, 2048)
    w2 = g[:, :, 5760:6784].reshape(128, 4, 4096).reshape(512, 4096)
    steps = lax.dynamic_slice_in_dim(g[:, :step_count, 6784:6784 + step_width], lax.axis_index("dp") * mp_size, mp_size, 0)
    steps = steps.transpose(1, 0, 2).reshape(step_count, mp_size * step_width)
    return w1, w2, w3, steps


def rms_scale(values, scales):
    widened = values.astype(jnp.float32)
    mean_square = jnp.mean(widened * widened, axis=-1, keepdims=True)
    return widened * lax.rsqrt(mean_square + NORM_EPS) * scales


def rotate(values, positions):
    rot_width = values.shape[-1]
    half_width = rot_width // 2
    freq_steps = jnp.arange(half_width, dtype=jnp.float32)
    inv_freqs = jnp.exp(freq_steps * (-2.0 * math.log(ROPE_BASE) / rot_width))
    angles = positions.astype(jnp.float32)[:, None] * inv_freqs[None, :]
    angle_shape = (positions.shape[0],) + (1,) * (values.ndim - 2) + (half_width,)
    cosine = jnp.cos(angles).reshape(angle_shape)
    sine_part = jnp.sin(angles).reshape(angle_shape)
    lower_half = values[..., :half_width]
    upper_half = values[..., half_width:]
    return jnp.concatenate(
        [
            lower_half * cosine - upper_half * sine_part,
            upper_half * cosine + lower_half * sine_part,
        ],
        axis=-1,
    )


def queries_keys(projected, positions, latent_gain, up_heads):
    head_cols = H * (DN + DR)
    row_count = projected.shape[0]
    query_cols = projected[:, :head_cols].reshape(row_count, H, DN + DR)
    query_rot = rotate(query_cols[..., DN:].astype(jnp.float32), positions).astype(jnp.bfloat16)
    latent = rms_scale(projected[:, head_cols : head_cols + LAT], latent_gain).astype(jnp.bfloat16)
    key_rot = rotate(projected[:, head_cols + LAT :].astype(jnp.float32), positions).astype(
        jnp.bfloat16
    )
    query_lat = jnp.einsum(
        "rhn,lhn->rhl", query_cols[..., :DN], up_heads[..., :DN], preferred_element_type=jnp.float32
    ).astype(jnp.bfloat16)
    queries = jnp.concatenate([query_lat, query_rot], axis=-1)
    key_rows = jnp.concatenate([latent, key_rot], axis=-1)
    return (queries, key_rows)


def prompt_attention(queries, query_ids, all_keys, all_ids, score_scale):
    row_count = queries.shape[0]
    block_rows = min(row_count, 512)
    block_count = row_count // block_rows
    query_blocks = queries.reshape(block_count, block_rows, H, queries.shape[-1])
    id_blocks = query_ids.reshape(block_count, block_rows)
    latent_keys = all_keys[:, :LAT]

    def one_block(block_args):
        query_part, id_part = block_args
        scores = (
            jnp.einsum("qhc,kc->qhk", query_part, all_keys, preferred_element_type=jnp.float32)
            * score_scale
        )
        same_prompt = id_part[:, None] // LEN == all_ids[None, :] // LEN
        allowed = same_prompt & (all_ids[None, :] <= id_part[:, None])
        scores = jnp.where(allowed[:, None, :], scores, MASKED)
        peak_score = jnp.max(scores, axis=-1, keepdims=True)
        weights = jnp.where(allowed[:, None, :], jnp.exp(scores - peak_score), 0.0)
        weight_sum = jnp.sum(weights, axis=-1, keepdims=True)
        summed = jnp.einsum(
            "qhk,kl->qhl",
            weights.astype(jnp.bfloat16),
            latent_keys,
            preferred_element_type=jnp.float32,
        )
        return (summed / weight_sum).astype(jnp.bfloat16)

    return lax.map(one_block, (query_blocks, id_blocks)).reshape(row_count, H, LAT)


def step_attention(queries, own_keys, latent_cache, page_table, cached_lengths, score_scale):
    pool = lax.all_gather(latent_cache, "mp", axis=0, tiled=True)
    request_count, page_count = page_table.shape
    page_rows = pool.shape[1]
    pages = pool[page_table].reshape(request_count, page_count * page_rows, pool.shape[2])
    key_all = jnp.concatenate([pages, own_keys[:, None, :]], axis=1)
    cached_ok = (
        jnp.arange(page_count * page_rows, dtype=jnp.int32)[None, :] < cached_lengths[:, None]
    )
    allowed = jnp.concatenate([cached_ok, jnp.ones((request_count, 1), jnp.bool_)], axis=1)
    scores = (
        jnp.einsum("rhc,rkc->rhk", queries, key_all, preferred_element_type=jnp.float32)
        * score_scale
    )
    scores = jnp.where(allowed[:, None, :], scores, MASKED)
    peak_score = jnp.max(scores, axis=-1, keepdims=True)
    weights = jnp.where(allowed[:, None, :], jnp.exp(scores - peak_score), 0.0)
    weight_sum = jnp.sum(weights, axis=-1, keepdims=True)
    summed = jnp.einsum(
        "rhk,rkl->rhl",
        weights.astype(jnp.bfloat16),
        key_all[:, :, :LAT],
        preferred_element_type=jnp.float32,
    )
    return (summed / weight_sum).astype(jnp.bfloat16)


def on_device(
    prompt_rows,
    step_rows,
    attn_gain,
    latent_gain,
    joined_qkva,
    kv_up,
    out_proj,
    latent_cache,
    page_table,
    cached_lengths,
):
    prompt_count = prompt_rows.shape[0]
    mp_index = lax.axis_index("mp")
    mp_size = lax.axis_size("mp")
    score_scale = (DN + DR) ** (-0.5)
    *served, step_full = gather_weights(joined_qkva, kv_up, out_proj, step_rows)
    served, latent_cache = lax.optimization_barrier((served, latent_cache))
    stacked = jnp.concatenate([prompt_rows, step_full], axis=0)
    normed = rms_scale(stacked, attn_gain).astype(jnp.bfloat16)
    prompt_ids = jnp.arange(prompt_count, dtype=jnp.int32)
    positions = jnp.concatenate([prompt_ids % LEN, cached_lengths], axis=0)
    inputs = normed
    projected = jnp.dot(
        inputs,
        served[0],
        preferred_element_type=jnp.float32,
    )
    up_heads = served[1].reshape(LAT, H, DN + DV)
    queries, key_rows = queries_keys(
        projected.astype(jnp.bfloat16), positions, latent_gain, up_heads
    )
    prompt_queries = queries[:prompt_count]
    prompt_key_rows = key_rows[:prompt_count]
    step_queries = queries[prompt_count:]
    step_keys = key_rows[prompt_count:]
    prompt_latent = prompt_attention(
        prompt_queries, prompt_ids, prompt_key_rows, prompt_ids, score_scale
    )
    step_latent = step_attention(
        step_queries, step_keys, latent_cache, page_table, cached_lengths, score_scale
    )
    latent_out = jnp.concatenate([prompt_latent, step_latent], axis=0)
    heads_out = jnp.einsum(
        "rhl,lhv->rhv", latent_out, up_heads[..., DN:], preferred_element_type=jnp.float32
    ).astype(jnp.bfloat16)
    heads_out = heads_out.reshape(latent_out.shape[0], H * DV)
    inputs = heads_out
    attended = jnp.dot(
        inputs,
        served[2],
        preferred_element_type=jnp.float32,
    )
    attended = attended.astype(jnp.bfloat16)
    prompt_out = attended[:prompt_count]
    col_width = attended.shape[1] // mp_size
    step_out = lax.dynamic_slice_in_dim(attended[prompt_count:], mp_index * col_width, col_width, 1)
    return (prompt_out, step_out)


def solution(mesh):
    placed = (
        P(("dp", "mp"), None),
        P("dp", "mp"),
        P(),
        P(),
        P("dp", "mp"),
        P("dp", "mp"),
        P("dp", "mp"),
        P(("dp", "mp"), None, None),
        P("dp", None),
        P("dp"),
    )
    return jax.shard_map(
        on_device,
        mesh=mesh,
        in_specs=placed,
        out_specs=(P(("dp", "mp"), None), P("dp", "mp")),
        check_vma=False,
    )
```

```python
import math

import numpy as np

import jax
import jax.numpy as jnp
from jax import lax
from jax.sharding import PartitionSpec as P

H = 16
DN = 128
DR = 64
DV = 128
LAT = 512
LEN = 512


NORM_EPS = 1e-06
ROPE_BASE = 50000.0
MASKED = -1e30


AXES = ("dp", "mp")


def _coords(i):
    dp, mp = i // 32, i % 32
    return (2 * (dp // 2) + (mp // 4) % 2, mp % 4, mp // 8, dp % 2)


def _index(x, y, z, core):
    return ((x // 2) * 2 + core) * 32 + z * 8 + (x % 2) * 4 + y


def _shift_pairs(dim, step):
    pairs = []
    for i in range(128):
        c = list(_coords(i))
        c[dim] = (c[dim] + step) % 4
        pairs.append((i, _index(*c)))
    return pairs


def torus_gather(block, cuts):
    rows = block.shape[0]
    partner = lax.ppermute(block, "dp", [(d, d ^ 1) for d in range(4)])
    chip = jnp.concatenate([block, partner], axis=0)
    me = lax.axis_index(AXES)
    dp, mp = me // 32, me % 32
    cx, cy, cz, ccore = 2 * (dp // 2) + (mp // 4) % 2, mp % 4, mp // 8, dp % 2
    ids = np.arange(128)
    x = 2 * (ids // 64) + (ids % 32 // 4) % 2
    y = ids % 4
    z = ids % 32 // 8
    core = (ids // 32) % 2
    rel = ((x - cx) % 4) * 16 + ((y - cy) % 4) * 4 + (z - cz) % 4
    pieces = []
    for part in range(len(cuts) - 1):
        data = chip[:, cuts[part]:cuts[part + 1]]
        offs = [(0, 0, 0)]
        for stage in range(3):
            dim = (part + stage) % 3
            right = lax.ppermute(data, AXES, _shift_pairs(dim, 1))
            left = lax.ppermute(data, AXES, _shift_pairs(dim, -1))
            far = lax.ppermute(right, AXES, _shift_pairs(dim, 1))
            new_offs = list(offs)
            for delta in (-1, 1, -2):
                for o in offs:
                    o = list(o)
                    o[dim] = (o[dim] + delta) % 4
                    new_offs.append(tuple(o))
            data = jnp.concatenate([data, right, left, far], axis=0)
            offs = new_offs
        table = np.zeros((4, 4, 4), np.int32)
        for pos, o in enumerate(offs):
            table[o] = pos
        pick = jnp.take(jnp.asarray(table.reshape(-1)), rel, mode="clip") * 2 + (core - ccore) % 2
        slabs = data.reshape(-1, rows, data.shape[-1])
        pieces.append(jnp.take(slabs, pick, axis=0, mode="clip"))
    return jnp.concatenate(pieces, axis=2)


def gather_weights(joined, kv_up, out_proj, step_rows, latent_cache):
    mp_size = 32
    j = joined.astype(jnp.bfloat16).reshape(mp_size, -1)
    k = kv_up.astype(jnp.bfloat16).reshape(mp_size, -1)
    o = out_proj.astype(jnp.bfloat16).reshape(mp_size, -1)
    cache = jnp.broadcast_to(latent_cache.reshape(1, -1), (mp_size, latent_cache.size))
    packed = jnp.concatenate([j, k, o, cache], axis=1)
    swapped = lax.all_to_all(packed, "mp", 0, 0, tiled=True)
    jw, kw = j.shape[1], k.shape[1]
    jr = swapped[:, :jw].reshape(mp_size, 16, 114).transpose(1, 0, 2).reshape(16, mp_size * 114)
    kr = swapped[:, jw:jw + kw].reshape(mp_size, 4, 128).transpose(1, 0, 2).reshape(16, 1024)
    ow = o.shape[1]
    pool = swapped[:, jw + kw + ow:].reshape((mp_size * latent_cache.shape[0],) + latent_cache.shape[1:])
    orr = swapped[:, jw + kw:jw + kw + ow].reshape(mp_size, 16, 64).transpose(1, 0, 2).reshape(16, mp_size * 64)
    jr = jnp.pad(jr, ((0, 0), (0, 3712 - 3648)))
    step_count, step_width = step_rows.shape
    step_block = jnp.pad(step_rows, ((0, 16 - step_count), (0, 128 - step_width)))
    block = jnp.concatenate([jr, orr, kr, step_block], axis=1)
    g = torus_gather(block, [0, 2304, 4608, 6912])
    w1 = g[:, :, :3648].reshape(2048, 3648)
    w3 = g[:, :, 3712:5760].reshape(2048, 2048)
    w2 = g[:, :, 5760:6784].reshape(128, 4, 4096).reshape(512, 4096)
    steps = lax.dynamic_slice_in_dim(g[:, :step_count, 6784:6784 + step_width], lax.axis_index("dp") * mp_size, mp_size, 0)
    steps = steps.transpose(1, 0, 2).reshape(step_count, mp_size * step_width)
    return w1, w2, w3, steps, pool


def rms_scale(values, scales):
    widened = values.astype(jnp.float32)
    mean_square = jnp.mean(widened * widened, axis=-1, keepdims=True)
    return widened * lax.rsqrt(mean_square + NORM_EPS) * scales


def rotate(values, positions):
    rot_width = values.shape[-1]
    half_width = rot_width // 2
    freq_steps = jnp.arange(half_width, dtype=jnp.float32)
    inv_freqs = jnp.exp(freq_steps * (-2.0 * math.log(ROPE_BASE) / rot_width))
    angles = positions.astype(jnp.float32)[:, None] * inv_freqs[None, :]
    angle_shape = (positions.shape[0],) + (1,) * (values.ndim - 2) + (half_width,)
    cosine = jnp.cos(angles).reshape(angle_shape)
    sine_part = jnp.sin(angles).reshape(angle_shape)
    lower_half = values[..., :half_width]
    upper_half = values[..., half_width:]
    return jnp.concatenate(
        [
            lower_half * cosine - upper_half * sine_part,
            upper_half * cosine + lower_half * sine_part,
        ],
        axis=-1,
    )


def queries_keys(projected, positions, latent_gain, up_heads):
    head_cols = H * (DN + DR)
    row_count = projected.shape[0]
    query_cols = projected[:, :head_cols].reshape(row_count, H, DN + DR)
    query_rot = rotate(query_cols[..., DN:].astype(jnp.float32), positions).astype(jnp.bfloat16)
    latent = rms_scale(projected[:, head_cols : head_cols + LAT], latent_gain).astype(jnp.bfloat16)
    key_rot = rotate(projected[:, head_cols + LAT :].astype(jnp.float32), positions).astype(
        jnp.bfloat16
    )
    query_lat = jnp.einsum(
        "rhn,lhn->rhl", query_cols[..., :DN], up_heads[..., :DN], preferred_element_type=jnp.float32
    ).astype(jnp.bfloat16)
    queries = jnp.concatenate([query_lat, query_rot], axis=-1)
    key_rows = jnp.concatenate([latent, key_rot], axis=-1)
    return (queries, key_rows)


def prompt_attention(queries, query_ids, all_keys, all_ids, score_scale):
    row_count = queries.shape[0]
    block_rows = min(row_count, 512)
    block_count = row_count // block_rows
    query_blocks = queries.reshape(block_count, block_rows, H, queries.shape[-1])
    id_blocks = query_ids.reshape(block_count, block_rows)
    latent_keys = all_keys[:, :LAT]

    def one_block(block_args):
        query_part, id_part = block_args
        scores = (
            jnp.einsum("qhc,kc->qhk", query_part, all_keys, preferred_element_type=jnp.float32)
            * score_scale
        )
        same_prompt = id_part[:, None] // LEN == all_ids[None, :] // LEN
        allowed = same_prompt & (all_ids[None, :] <= id_part[:, None])
        scores = jnp.where(allowed[:, None, :], scores, MASKED)
        peak_score = jnp.max(scores, axis=-1, keepdims=True)
        weights = jnp.where(allowed[:, None, :], jnp.exp(scores - peak_score), 0.0)
        weight_sum = jnp.sum(weights, axis=-1, keepdims=True)
        summed = jnp.einsum(
            "qhk,kl->qhl",
            weights.astype(jnp.bfloat16),
            latent_keys,
            preferred_element_type=jnp.float32,
        )
        return (summed / weight_sum).astype(jnp.bfloat16)

    return lax.map(one_block, (query_blocks, id_blocks)).reshape(row_count, H, LAT)


def step_attention(queries, own_keys, pool, page_table, cached_lengths, score_scale):
    request_count, page_count = page_table.shape
    page_rows = pool.shape[1]
    pages = pool[page_table].reshape(request_count, page_count * page_rows, pool.shape[2])
    key_all = jnp.concatenate([pages, own_keys[:, None, :]], axis=1)
    cached_ok = (
        jnp.arange(page_count * page_rows, dtype=jnp.int32)[None, :] < cached_lengths[:, None]
    )
    allowed = jnp.concatenate([cached_ok, jnp.ones((request_count, 1), jnp.bool_)], axis=1)
    scores = (
        jnp.einsum("rhc,rkc->rhk", queries, key_all, preferred_element_type=jnp.float32)
        * score_scale
    )
    scores = jnp.where(allowed[:, None, :], scores, MASKED)
    peak_score = jnp.max(scores, axis=-1, keepdims=True)
    weights = jnp.where(allowed[:, None, :], jnp.exp(scores - peak_score), 0.0)
    weight_sum = jnp.sum(weights, axis=-1, keepdims=True)
    summed = jnp.einsum(
        "rhk,rkl->rhl",
        weights.astype(jnp.bfloat16),
        key_all[:, :, :LAT],
        preferred_element_type=jnp.float32,
    )
    return (summed / weight_sum).astype(jnp.bfloat16)


def on_device(
    prompt_rows,
    step_rows,
    attn_gain,
    latent_gain,
    joined_qkva,
    kv_up,
    out_proj,
    latent_cache,
    page_table,
    cached_lengths,
):
    prompt_count = prompt_rows.shape[0]
    mp_index = lax.axis_index("mp")
    mp_size = lax.axis_size("mp")
    score_scale = (DN + DR) ** (-0.5)
    *served, step_full, pool = gather_weights(joined_qkva, kv_up, out_proj, step_rows, latent_cache)
    stacked = jnp.concatenate([prompt_rows, step_full], axis=0)
    normed = rms_scale(stacked, attn_gain).astype(jnp.bfloat16)
    prompt_ids = jnp.arange(prompt_count, dtype=jnp.int32)
    positions = jnp.concatenate([prompt_ids % LEN, cached_lengths], axis=0)
    inputs = normed
    projected = jnp.dot(
        inputs,
        served[0],
        preferred_element_type=jnp.float32,
    )
    up_heads = served[1].reshape(LAT, H, DN + DV)
    queries, key_rows = queries_keys(
        projected.astype(jnp.bfloat16), positions, latent_gain, up_heads
    )
    prompt_queries = queries[:prompt_count]
    prompt_key_rows = key_rows[:prompt_count]
    step_queries = queries[prompt_count:]
    step_keys = key_rows[prompt_count:]
    prompt_latent = prompt_attention(
        prompt_queries, prompt_ids, prompt_key_rows, prompt_ids, score_scale
    )
    step_latent = step_attention(
        step_queries, step_keys, pool, page_table, cached_lengths, score_scale
    )
    latent_out = jnp.concatenate([prompt_latent, step_latent], axis=0)
    heads_out = jnp.einsum(
        "rhl,lhv->rhv", latent_out, up_heads[..., DN:], preferred_element_type=jnp.float32
    ).astype(jnp.bfloat16)
    heads_out = heads_out.reshape(latent_out.shape[0], H * DV)
    inputs = heads_out
    attended = jnp.dot(
        inputs,
        served[2],
        preferred_element_type=jnp.float32,
    )
    attended = attended.astype(jnp.bfloat16)
    prompt_out = attended[:prompt_count]
    col_width = attended.shape[1] // mp_size
    step_out = lax.dynamic_slice_in_dim(attended[prompt_count:], mp_index * col_width, col_width, 1)
    return (prompt_out, step_out)


def solution(mesh):
    placed = (
        P(("dp", "mp"), None),
        P("dp", "mp"),
        P(),
        P(),
        P("dp", "mp"),
        P("dp", "mp"),
        P("dp", "mp"),
        P(("dp", "mp"), None, None),
        P("dp", None),
        P("dp"),
    )
    return jax.shard_map(
        on_device,
        mesh=mesh,
        in_specs=placed,
        out_specs=(P(("dp", "mp"), None), P("dp", "mp")),
        check_vma=False,
    )
```

```python
import math

import numpy as np

import jax
import jax.numpy as jnp
from jax import lax
from jax.sharding import PartitionSpec as P

H = 16
DN = 128
DR = 64
DV = 128
LAT = 512
LEN = 512


NORM_EPS = 1e-06
ROPE_BASE = 50000.0
MASKED = -1e30


AXES = ("dp", "mp")


def _coords(i):
    dp, mp = i // 32, i % 32
    return (2 * (dp // 2) + (mp // 4) % 2, mp % 4, mp // 8, dp % 2)


def _index(x, y, z, core):
    return ((x // 2) * 2 + core) * 32 + z * 8 + (x % 2) * 4 + y


def _shift_pairs(dim, step):
    pairs = []
    for i in range(128):
        c = list(_coords(i))
        c[dim] = (c[dim] + step) % 4
        pairs.append((i, _index(*c)))
    return pairs


def torus_gather(block, cuts):
    rows = block.shape[0]
    partner = lax.ppermute(block, "dp", [(d, d ^ 1) for d in range(4)])
    chip = jnp.concatenate([block, partner], axis=0)
    me = lax.axis_index(AXES)
    dp, mp = me // 32, me % 32
    cx, cy, cz, ccore = 2 * (dp // 2) + (mp // 4) % 2, mp % 4, mp // 8, dp % 2
    ids = np.arange(128)
    x = 2 * (ids // 64) + (ids % 32 // 4) % 2
    y = ids % 4
    z = ids % 32 // 8
    core = (ids // 32) % 2
    rel = ((x - cx) % 4) * 16 + ((y - cy) % 4) * 4 + (z - cz) % 4
    pieces = []
    for part in range(len(cuts) - 1):
        data = chip[:, cuts[part]:cuts[part + 1]]
        offs = [(0, 0, 0)]
        for stage in range(3):
            dim = (part + stage) % 3
            right = lax.ppermute(data, AXES, _shift_pairs(dim, 1))
            left = lax.ppermute(data, AXES, _shift_pairs(dim, -1))
            far = lax.ppermute(data, AXES, _shift_pairs(dim, 2))
            new_offs = list(offs)
            for delta in (-1, 1, -2):
                for o in offs:
                    o = list(o)
                    o[dim] = (o[dim] + delta) % 4
                    new_offs.append(tuple(o))
            data = jnp.concatenate([data, right, left, far], axis=0)
            offs = new_offs
        table = np.zeros((4, 4, 4), np.int32)
        for pos, o in enumerate(offs):
            table[o] = pos
        pick = jnp.take(jnp.asarray(table.reshape(-1)), rel, mode="clip") * 2 + (core - ccore) % 2
        slabs = data.reshape(-1, rows, data.shape[-1])
        pieces.append(jnp.take(slabs, pick, axis=0, mode="clip"))
    return jnp.concatenate(pieces, axis=2)


def gather_weights(joined, kv_up, out_proj, step_rows, latent_cache):
    mp_size = 32
    j = joined.astype(jnp.bfloat16).reshape(mp_size, -1)
    k = kv_up.astype(jnp.bfloat16).reshape(mp_size, -1)
    o = out_proj.astype(jnp.bfloat16).reshape(mp_size, -1)
    cache = jnp.broadcast_to(latent_cache.reshape(1, -1), (mp_size, latent_cache.size))
    packed = jnp.concatenate([j, k, o, cache], axis=1)
    swapped = lax.all_to_all(packed, "mp", 0, 0, tiled=True)
    jw, kw = j.shape[1], k.shape[1]
    jr = swapped[:, :jw].reshape(mp_size, 16, 114).transpose(1, 0, 2).reshape(16, mp_size * 114)
    kr = swapped[:, jw:jw + kw].reshape(mp_size, 4, 128).transpose(1, 0, 2).reshape(16, 1024)
    ow = o.shape[1]
    pool = swapped[:, jw + kw + ow:].reshape((mp_size * latent_cache.shape[0],) + latent_cache.shape[1:])
    orr = swapped[:, jw + kw:jw + kw + ow].reshape(mp_size, 16, 64).transpose(1, 0, 2).reshape(16, mp_size * 64)
    jr = jnp.pad(jr, ((0, 0), (0, 3712 - 3648)))
    step_count, step_width = step_rows.shape
    step_block = jnp.pad(step_rows, ((0, 16 - step_count), (0, 128 - step_width)))
    block = jnp.concatenate([jr, orr, kr, step_block], axis=1)
    g = torus_gather(block, [0, 2304, 4608, 6912])
    w1 = g[:, :, :3648].reshape(2048, 3648)
    w3 = g[:, :, 3712:5760].reshape(2048, 2048)
    w2 = g[:, :, 5760:6784].reshape(128, 4, 4096).reshape(512, 4096)
    steps = lax.dynamic_slice_in_dim(g[:, :step_count, 6784:6784 + step_width], lax.axis_index("dp") * mp_size, mp_size, 0)
    steps = steps.transpose(1, 0, 2).reshape(step_count, mp_size * step_width)
    return w1, w2, w3, steps, pool


def rms_scale(values, scales):
    widened = values.astype(jnp.float32)
    mean_square = jnp.mean(widened * widened, axis=-1, keepdims=True)
    return widened * lax.rsqrt(mean_square + NORM_EPS) * scales


def rotate(values, positions):
    rot_width = values.shape[-1]
    half_width = rot_width // 2
    freq_steps = jnp.arange(half_width, dtype=jnp.float32)
    inv_freqs = jnp.exp(freq_steps * (-2.0 * math.log(ROPE_BASE) / rot_width))
    angles = positions.astype(jnp.float32)[:, None] * inv_freqs[None, :]
    angle_shape = (positions.shape[0],) + (1,) * (values.ndim - 2) + (half_width,)
    cosine = jnp.cos(angles).reshape(angle_shape)
    sine_part = jnp.sin(angles).reshape(angle_shape)
    lower_half = values[..., :half_width]
    upper_half = values[..., half_width:]
    return jnp.concatenate(
        [
            lower_half * cosine - upper_half * sine_part,
            upper_half * cosine + lower_half * sine_part,
        ],
        axis=-1,
    )


def queries_keys(projected, positions, latent_gain, up_heads):
    head_cols = H * (DN + DR)
    row_count = projected.shape[0]
    query_cols = projected[:, :head_cols].reshape(row_count, H, DN + DR)
    query_rot = rotate(query_cols[..., DN:].astype(jnp.float32), positions).astype(jnp.bfloat16)
    latent = rms_scale(projected[:, head_cols : head_cols + LAT], latent_gain).astype(jnp.bfloat16)
    key_rot = rotate(projected[:, head_cols + LAT :].astype(jnp.float32), positions).astype(
        jnp.bfloat16
    )
    query_lat = jnp.einsum(
        "rhn,lhn->rhl", query_cols[..., :DN], up_heads[..., :DN], preferred_element_type=jnp.float32
    ).astype(jnp.bfloat16)
    queries = jnp.concatenate([query_lat, query_rot], axis=-1)
    key_rows = jnp.concatenate([latent, key_rot], axis=-1)
    return (queries, key_rows)


def prompt_attention(queries, query_ids, all_keys, all_ids, score_scale):
    row_count = queries.shape[0]
    block_rows = min(row_count, 512)
    block_count = row_count // block_rows
    query_blocks = queries.reshape(block_count, block_rows, H, queries.shape[-1])
    id_blocks = query_ids.reshape(block_count, block_rows)
    latent_keys = all_keys[:, :LAT]

    def one_block(block_args):
        query_part, id_part = block_args
        scores = (
            jnp.einsum("qhc,kc->qhk", query_part, all_keys, preferred_element_type=jnp.float32)
            * score_scale
        )
        same_prompt = id_part[:, None] // LEN == all_ids[None, :] // LEN
        allowed = same_prompt & (all_ids[None, :] <= id_part[:, None])
        scores = jnp.where(allowed[:, None, :], scores, MASKED)
        peak_score = jnp.max(scores, axis=-1, keepdims=True)
        weights = jnp.where(allowed[:, None, :], jnp.exp(scores - peak_score), 0.0)
        weight_sum = jnp.sum(weights, axis=-1, keepdims=True)
        summed = jnp.einsum(
            "qhk,kl->qhl",
            weights.astype(jnp.bfloat16),
            latent_keys,
            preferred_element_type=jnp.float32,
        )
        return (summed / weight_sum).astype(jnp.bfloat16)

    return lax.map(one_block, (query_blocks, id_blocks)).reshape(row_count, H, LAT)


def step_attention(queries, own_keys, pool, page_table, cached_lengths, score_scale):
    request_count, page_count = page_table.shape
    page_rows = pool.shape[1]
    pages = pool[page_table].reshape(request_count, page_count * page_rows, pool.shape[2])
    key_all = jnp.concatenate([pages, own_keys[:, None, :]], axis=1)
    cached_ok = (
        jnp.arange(page_count * page_rows, dtype=jnp.int32)[None, :] < cached_lengths[:, None]
    )
    allowed = jnp.concatenate([cached_ok, jnp.ones((request_count, 1), jnp.bool_)], axis=1)
    scores = (
        jnp.einsum("rhc,rkc->rhk", queries, key_all, preferred_element_type=jnp.float32)
        * score_scale
    )
    scores = jnp.where(allowed[:, None, :], scores, MASKED)
    peak_score = jnp.max(scores, axis=-1, keepdims=True)
    weights = jnp.where(allowed[:, None, :], jnp.exp(scores - peak_score), 0.0)
    weight_sum = jnp.sum(weights, axis=-1, keepdims=True)
    summed = jnp.einsum(
        "rhk,rkl->rhl",
        weights.astype(jnp.bfloat16),
        key_all[:, :, :LAT],
        preferred_element_type=jnp.float32,
    )
    return (summed / weight_sum).astype(jnp.bfloat16)


def on_device(
    prompt_rows,
    step_rows,
    attn_gain,
    latent_gain,
    joined_qkva,
    kv_up,
    out_proj,
    latent_cache,
    page_table,
    cached_lengths,
):
    prompt_count = prompt_rows.shape[0]
    mp_index = lax.axis_index("mp")
    mp_size = lax.axis_size("mp")
    score_scale = (DN + DR) ** (-0.5)
    *served, step_full, pool = gather_weights(joined_qkva, kv_up, out_proj, step_rows, latent_cache)
    stacked = jnp.concatenate([prompt_rows, step_full], axis=0)
    normed = rms_scale(stacked, attn_gain).astype(jnp.bfloat16)
    prompt_ids = jnp.arange(prompt_count, dtype=jnp.int32)
    positions = jnp.concatenate([prompt_ids % LEN, cached_lengths], axis=0)
    inputs = normed
    projected = jnp.dot(
        inputs,
        served[0],
        preferred_element_type=jnp.float32,
    )
    up_heads = served[1].reshape(LAT, H, DN + DV)
    queries, key_rows = queries_keys(
        projected.astype(jnp.bfloat16), positions, latent_gain, up_heads
    )
    prompt_queries = queries[:prompt_count]
    prompt_key_rows = key_rows[:prompt_count]
    step_queries = queries[prompt_count:]
    step_keys = key_rows[prompt_count:]
    prompt_latent = prompt_attention(
        prompt_queries, prompt_ids, prompt_key_rows, prompt_ids, score_scale
    )
    step_latent = step_attention(
        step_queries, step_keys, pool, page_table, cached_lengths, score_scale
    )
    latent_out = jnp.concatenate([prompt_latent, step_latent], axis=0)
    heads_out = jnp.einsum(
        "rhl,lhv->rhv", latent_out, up_heads[..., DN:], preferred_element_type=jnp.float32
    ).astype(jnp.bfloat16)
    heads_out = heads_out.reshape(latent_out.shape[0], H * DV)
    inputs = heads_out
    attended = jnp.dot(
        inputs,
        served[2],
        preferred_element_type=jnp.float32,
    )
    attended = attended.astype(jnp.bfloat16)
    prompt_out = attended[:prompt_count]
    col_width = attended.shape[1] // mp_size
    step_out = lax.dynamic_slice_in_dim(attended[prompt_count:], mp_index * col_width, col_width, 1)
    return (prompt_out, step_out)


def solution(mesh):
    placed = (
        P(("dp", "mp"), None),
        P("dp", "mp"),
        P(),
        P(),
        P("dp", "mp"),
        P("dp", "mp"),
        P("dp", "mp"),
        P(("dp", "mp"), None, None),
        P("dp", None),
        P("dp"),
    )
    return jax.shard_map(
        on_device,
        mesh=mesh,
        in_specs=placed,
        out_specs=(P(("dp", "mp"), None), P("dp", "mp")),
        check_vma=False,
    )
```

```python
import math

import numpy as np

import jax
import jax.numpy as jnp
from jax import lax
from jax.sharding import PartitionSpec as P

H = 16
DN = 128
DR = 64
DV = 128
LAT = 512
LEN = 512


NORM_EPS = 1e-06
ROPE_BASE = 50000.0
MASKED = -1e30


AXES = ("dp", "mp")


def _coords(i):
    dp, mp = i // 32, i % 32
    return (2 * (dp // 2) + (mp // 4) % 2, mp % 4, mp // 8, dp % 2)


def _index(x, y, z, core):
    return ((x // 2) * 2 + core) * 32 + z * 8 + (x % 2) * 4 + y


def _shift_pairs(dim, step):
    pairs = []
    for i in range(128):
        c = list(_coords(i))
        c[dim] = (c[dim] + step) % 4
        pairs.append((i, _index(*c)))
    return pairs


def torus_gather(block, cuts):
    rows = block.shape[0]
    me = lax.axis_index(AXES)
    dp, mp = me // 32, me % 32
    cx, cy, cz, ccore = 2 * (dp // 2) + (mp // 4) % 2, mp % 4, mp // 8, dp % 2
    ids = np.arange(128)
    x = 2 * (ids // 64) + (ids % 32 // 4) % 2
    y = ids % 4
    z = ids % 32 // 8
    core = (ids // 32) % 2
    rel = ((x - cx) % 4) * 16 + ((y - cy) % 4) * 4 + (z - cz) % 4
    pieces = []
    for part in range(len(cuts) - 1):
        data = block[:, cuts[part]:cuts[part + 1]]
        offs = [(0, 0, 0)]
        for stage in range(3):
            dim = (part + stage) % 3
            right = lax.ppermute(data, AXES, _shift_pairs(dim, 1))
            left = lax.ppermute(data, AXES, _shift_pairs(dim, -1))
            far = lax.ppermute(right, AXES, _shift_pairs(dim, 1))
            new_offs = list(offs)
            for delta in (-1, 1, -2):
                for o in offs:
                    o = list(o)
                    o[dim] = (o[dim] + delta) % 4
                    new_offs.append(tuple(o))
            data = jnp.concatenate([data, right, left, far], axis=0)
            offs = new_offs
        table = np.zeros((4, 4, 4), np.int32)
        for pos, o in enumerate(offs):
            table[o] = pos
        pick = jnp.take(jnp.asarray(table.reshape(-1)), rel, mode="clip") + (core - ccore) % 2 * 64
        partner = lax.ppermute(data, "dp", [(d, d ^ 1) for d in range(4)])
        slabs = jnp.concatenate([data, partner], axis=0).reshape(-1, rows, data.shape[-1])
        pieces.append(jnp.take(slabs, pick, axis=0, mode="clip"))
    return jnp.concatenate(pieces, axis=2)


def gather_weights(joined, kv_up, out_proj, step_rows, latent_cache):
    mp_size = 32
    j = joined.astype(jnp.bfloat16).reshape(mp_size, -1)
    k = kv_up.astype(jnp.bfloat16).reshape(mp_size, -1)
    o = out_proj.astype(jnp.bfloat16).reshape(mp_size, -1)
    cache = jnp.broadcast_to(latent_cache.reshape(1, -1), (mp_size, latent_cache.size))
    packed = jnp.concatenate([j, k, o, cache], axis=1)
    swapped = lax.all_to_all(packed, "mp", 0, 0, tiled=True)
    jw, kw = j.shape[1], k.shape[1]
    jr = swapped[:, :jw].reshape(mp_size, 16, 114).transpose(1, 0, 2).reshape(16, mp_size * 114)
    kr = swapped[:, jw:jw + kw].reshape(mp_size, 4, 128).transpose(1, 0, 2).reshape(16, 1024)
    ow = o.shape[1]
    pool = swapped[:, jw + kw + ow:].reshape((mp_size * latent_cache.shape[0],) + latent_cache.shape[1:])
    orr = swapped[:, jw + kw:jw + kw + ow].reshape(mp_size, 16, 64).transpose(1, 0, 2).reshape(16, mp_size * 64)
    jr = jnp.pad(jr, ((0, 0), (0, 3712 - 3648)))
    step_count, step_width = step_rows.shape
    step_block = jnp.pad(step_rows, ((0, 16 - step_count), (0, 128 - step_width)))
    block = jnp.concatenate([jr, orr, kr, step_block], axis=1)
    g = torus_gather(block, [0, 2304, 4608, 6912])
    w1 = g[:, :, :3648].reshape(2048, 3648)
    w3 = g[:, :, 3712:5760].reshape(2048, 2048)
    w2 = g[:, :, 5760:6784].reshape(128, 4, 4096).reshape(512, 4096)
    steps = lax.dynamic_slice_in_dim(g[:, :step_count, 6784:6784 + step_width], lax.axis_index("dp") * mp_size, mp_size, 0)
    steps = steps.transpose(1, 0, 2).reshape(step_count, mp_size * step_width)
    return w1, w2, w3, steps, pool


def rms_scale(values, scales):
    widened = values.astype(jnp.float32)
    mean_square = jnp.mean(widened * widened, axis=-1, keepdims=True)
    return widened * lax.rsqrt(mean_square + NORM_EPS) * scales


def rotate(values, positions):
    rot_width = values.shape[-1]
    half_width = rot_width // 2
    freq_steps = jnp.arange(half_width, dtype=jnp.float32)
    inv_freqs = jnp.exp(freq_steps * (-2.0 * math.log(ROPE_BASE) / rot_width))
    angles = positions.astype(jnp.float32)[:, None] * inv_freqs[None, :]
    angle_shape = (positions.shape[0],) + (1,) * (values.ndim - 2) + (half_width,)
    cosine = jnp.cos(angles).reshape(angle_shape)
    sine_part = jnp.sin(angles).reshape(angle_shape)
    lower_half = values[..., :half_width]
    upper_half = values[..., half_width:]
    return jnp.concatenate(
        [
            lower_half * cosine - upper_half * sine_part,
            upper_half * cosine + lower_half * sine_part,
        ],
        axis=-1,
    )


def queries_keys(projected, positions, latent_gain, up_heads):
    head_cols = H * (DN + DR)
    row_count = projected.shape[0]
    query_cols = projected[:, :head_cols].reshape(row_count, H, DN + DR)
    query_rot = rotate(query_cols[..., DN:].astype(jnp.float32), positions).astype(jnp.bfloat16)
    latent = rms_scale(projected[:, head_cols : head_cols + LAT], latent_gain).astype(jnp.bfloat16)
    key_rot = rotate(projected[:, head_cols + LAT :].astype(jnp.float32), positions).astype(
        jnp.bfloat16
    )
    query_lat = jnp.einsum(
        "rhn,lhn->rhl", query_cols[..., :DN], up_heads[..., :DN], preferred_element_type=jnp.float32
    ).astype(jnp.bfloat16)
    queries = jnp.concatenate([query_lat, query_rot], axis=-1)
    key_rows = jnp.concatenate([latent, key_rot], axis=-1)
    return (queries, key_rows)


def prompt_attention(queries, query_ids, all_keys, all_ids, score_scale):
    row_count = queries.shape[0]
    block_rows = min(row_count, 512)
    block_count = row_count // block_rows
    query_blocks = queries.reshape(block_count, block_rows, H, queries.shape[-1])
    id_blocks = query_ids.reshape(block_count, block_rows)
    latent_keys = all_keys[:, :LAT]

    def one_block(block_args):
        query_part, id_part = block_args
        scores = (
            jnp.einsum("qhc,kc->qhk", query_part, all_keys, preferred_element_type=jnp.float32)
            * score_scale
        )
        same_prompt = id_part[:, None] // LEN == all_ids[None, :] // LEN
        allowed = same_prompt & (all_ids[None, :] <= id_part[:, None])
        scores = jnp.where(allowed[:, None, :], scores, MASKED)
        peak_score = jnp.max(scores, axis=-1, keepdims=True)
        weights = jnp.where(allowed[:, None, :], jnp.exp(scores - peak_score), 0.0)
        weight_sum = jnp.sum(weights, axis=-1, keepdims=True)
        summed = jnp.einsum(
            "qhk,kl->qhl",
            weights.astype(jnp.bfloat16),
            latent_keys,
            preferred_element_type=jnp.float32,
        )
        return (summed / weight_sum).astype(jnp.bfloat16)

    return lax.map(one_block, (query_blocks, id_blocks)).reshape(row_count, H, LAT)


def step_attention(queries, own_keys, pool, page_table, cached_lengths, score_scale):
    request_count, page_count = page_table.shape
    page_rows = pool.shape[1]
    pages = pool[page_table].reshape(request_count, page_count * page_rows, pool.shape[2])
    key_all = jnp.concatenate([pages, own_keys[:, None, :]], axis=1)
    cached_ok = (
        jnp.arange(page_count * page_rows, dtype=jnp.int32)[None, :] < cached_lengths[:, None]
    )
    allowed = jnp.concatenate([cached_ok, jnp.ones((request_count, 1), jnp.bool_)], axis=1)
    scores = (
        jnp.einsum("rhc,rkc->rhk", queries, key_all, preferred_element_type=jnp.float32)
        * score_scale
    )
    scores = jnp.where(allowed[:, None, :], scores, MASKED)
    peak_score = jnp.max(scores, axis=-1, keepdims=True)
    weights = jnp.where(allowed[:, None, :], jnp.exp(scores - peak_score), 0.0)
    weight_sum = jnp.sum(weights, axis=-1, keepdims=True)
    summed = jnp.einsum(
        "rhk,rkl->rhl",
        weights.astype(jnp.bfloat16),
        key_all[:, :, :LAT],
        preferred_element_type=jnp.float32,
    )
    return (summed / weight_sum).astype(jnp.bfloat16)


def on_device(
    prompt_rows,
    step_rows,
    attn_gain,
    latent_gain,
    joined_qkva,
    kv_up,
    out_proj,
    latent_cache,
    page_table,
    cached_lengths,
):
    prompt_count = prompt_rows.shape[0]
    mp_index = lax.axis_index("mp")
    mp_size = lax.axis_size("mp")
    score_scale = (DN + DR) ** (-0.5)
    *served, step_full, pool = gather_weights(joined_qkva, kv_up, out_proj, step_rows, latent_cache)
    stacked = jnp.concatenate([prompt_rows, step_full], axis=0)
    normed = rms_scale(stacked, attn_gain).astype(jnp.bfloat16)
    prompt_ids = jnp.arange(prompt_count, dtype=jnp.int32)
    positions = jnp.concatenate([prompt_ids % LEN, cached_lengths], axis=0)
    inputs = normed
    projected = jnp.dot(
        inputs,
        served[0],
        preferred_element_type=jnp.float32,
    )
    up_heads = served[1].reshape(LAT, H, DN + DV)
    queries, key_rows = queries_keys(
        projected.astype(jnp.bfloat16), positions, latent_gain, up_heads
    )
    prompt_queries = queries[:prompt_count]
    prompt_key_rows = key_rows[:prompt_count]
    step_queries = queries[prompt_count:]
    step_keys = key_rows[prompt_count:]
    prompt_latent = prompt_attention(
        prompt_queries, prompt_ids, prompt_key_rows, prompt_ids, score_scale
    )
    step_latent = step_attention(
        step_queries, step_keys, pool, page_table, cached_lengths, score_scale
    )
    latent_out = jnp.concatenate([prompt_latent, step_latent], axis=0)
    heads_out = jnp.einsum(
        "rhl,lhv->rhv", latent_out, up_heads[..., DN:], preferred_element_type=jnp.float32
    ).astype(jnp.bfloat16)
    heads_out = heads_out.reshape(latent_out.shape[0], H * DV)
    inputs = heads_out
    attended = jnp.dot(
        inputs,
        served[2],
        preferred_element_type=jnp.float32,
    )
    attended = attended.astype(jnp.bfloat16)
    prompt_out = attended[:prompt_count]
    col_width = attended.shape[1] // mp_size
    step_out = lax.dynamic_slice_in_dim(attended[prompt_count:], mp_index * col_width, col_width, 1)
    return (prompt_out, step_out)


def solution(mesh):
    placed = (
        P(("dp", "mp"), None),
        P("dp", "mp"),
        P(),
        P(),
        P("dp", "mp"),
        P("dp", "mp"),
        P("dp", "mp"),
        P(("dp", "mp"), None, None),
        P("dp", None),
        P("dp"),
    )
    return jax.shard_map(
        on_device,
        mesh=mesh,
        in_specs=placed,
        out_specs=(P(("dp", "mp"), None), P("dp", "mp")),
        check_vma=False,
    )
```

```python
import math

import numpy as np

import jax
import jax.numpy as jnp
from jax import lax
from jax.sharding import PartitionSpec as P

H = 16
DN = 128
DR = 64
DV = 128
LAT = 512
LEN = 512


NORM_EPS = 1e-06
ROPE_BASE = 50000.0
MASKED = -1e30


AXES = ("dp", "mp")


def _coords(i):
    dp, mp = i // 32, i % 32
    return (2 * (dp // 2) + (mp // 4) % 2, mp % 4, mp // 8, dp % 2)


def _index(x, y, z, core):
    return ((x // 2) * 2 + core) * 32 + z * 8 + (x % 2) * 4 + y


def _shift_pairs(dim, step):
    pairs = []
    for i in range(128):
        c = list(_coords(i))
        c[dim] = (c[dim] + step) % 4
        pairs.append((i, _index(*c)))
    return pairs


def torus_gather(block, cuts):
    rows = block.shape[0]
    me = lax.axis_index(AXES)
    dp, mp = me // 32, me % 32
    cx, cy, cz, ccore = 2 * (dp // 2) + (mp // 4) % 2, mp % 4, mp // 8, dp % 2
    ids = np.arange(128)
    x = 2 * (ids // 64) + (ids % 32 // 4) % 2
    y = ids % 4
    z = ids % 32 // 8
    core = (ids // 32) % 2
    rel = ((x - cx) % 4) * 16 + ((y - cy) % 4) * 4 + (z - cz) % 4
    pieces = []
    for part in range(len(cuts) - 1):
        data = block[:, cuts[part]:cuts[part + 1]]
        offs = [(0, 0, 0)]
        for stage in range(3):
            dim = (part + stage) % 3
            right = lax.ppermute(data, AXES, _shift_pairs(dim, 1))
            left = lax.ppermute(data, AXES, _shift_pairs(dim, -1))
            far = lax.ppermute(right, AXES, _shift_pairs(dim, 1))
            new_offs = list(offs)
            for delta in (-1, 1, -2):
                for o in offs:
                    o = list(o)
                    o[dim] = (o[dim] + delta) % 4
                    new_offs.append(tuple(o))
            data = jnp.concatenate([data, right, left, far], axis=0)
            offs = new_offs
        table = np.zeros((4, 4, 4), np.int32)
        for pos, o in enumerate(offs):
            table[o] = pos
        pick = jnp.take(jnp.asarray(table.reshape(-1)), rel, mode="clip") + (core - ccore) % 2 * 64
        partner = lax.ppermute(data, "dp", [(d, d ^ 1) for d in range(4)])
        slabs = jnp.concatenate([data, partner], axis=0).reshape(-1, rows, data.shape[-1])
        pieces.append(jnp.take(slabs, pick, axis=0, mode="clip"))
    return jnp.concatenate(pieces, axis=2)


def gather_weights(joined, kv_up, out_proj, step_rows, latent_cache):
    mp_size = 32
    j = joined.astype(jnp.bfloat16).reshape(mp_size, -1)
    k = kv_up.astype(jnp.bfloat16).reshape(mp_size, -1)
    o = out_proj.astype(jnp.bfloat16).reshape(mp_size, -1)
    cache = jnp.broadcast_to(latent_cache.reshape(1, -1), (mp_size, latent_cache.size))
    packed = jnp.concatenate([j, k, o], axis=1)
    swapped = lax.all_to_all(packed, "mp", 0, 0, tiled=True)
    jw, kw = j.shape[1], k.shape[1]
    jr = swapped[:, :jw].reshape(mp_size, 16, 114).transpose(1, 0, 2).reshape(16, mp_size * 114)
    kr = swapped[:, jw:jw + kw].reshape(mp_size, 4, 128).transpose(1, 0, 2).reshape(16, 1024)
    ow = o.shape[1]
    pool = lax.all_to_all(cache, "mp", 0, 0, tiled=True).reshape((mp_size * latent_cache.shape[0],) + latent_cache.shape[1:])
    orr = swapped[:, jw + kw:jw + kw + ow].reshape(mp_size, 16, 64).transpose(1, 0, 2).reshape(16, mp_size * 64)
    jr = jnp.pad(jr, ((0, 0), (0, 3712 - 3648)))
    step_count, step_width = step_rows.shape
    step_block = jnp.pad(step_rows, ((0, 16 - step_count), (0, 128 - step_width)))
    block = jnp.concatenate([jr, orr, kr, step_block], axis=1)
    g = torus_gather(block, [0, 2304, 4608, 6912])
    w1 = g[:, :, :3648].reshape(2048, 3648)
    w3 = g[:, :, 3712:5760].reshape(2048, 2048)
    w2 = g[:, :, 5760:6784].reshape(128, 4, 4096).reshape(512, 4096)
    steps = lax.dynamic_slice_in_dim(g[:, :step_count, 6784:6784 + step_width], lax.axis_index("dp") * mp_size, mp_size, 0)
    steps = steps.transpose(1, 0, 2).reshape(step_count, mp_size * step_width)
    return w1, w2, w3, steps, pool


def rms_scale(values, scales):
    widened = values.astype(jnp.float32)
    mean_square = jnp.mean(widened * widened, axis=-1, keepdims=True)
    return widened * lax.rsqrt(mean_square + NORM_EPS) * scales


def rotate(values, positions):
    rot_width = values.shape[-1]
    half_width = rot_width // 2
    freq_steps = jnp.arange(half_width, dtype=jnp.float32)
    inv_freqs = jnp.exp(freq_steps * (-2.0 * math.log(ROPE_BASE) / rot_width))
    angles = positions.astype(jnp.float32)[:, None] * inv_freqs[None, :]
    angle_shape = (positions.shape[0],) + (1,) * (values.ndim - 2) + (half_width,)
    cosine = jnp.cos(angles).reshape(angle_shape)
    sine_part = jnp.sin(angles).reshape(angle_shape)
    lower_half = values[..., :half_width]
    upper_half = values[..., half_width:]
    return jnp.concatenate(
        [
            lower_half * cosine - upper_half * sine_part,
            upper_half * cosine + lower_half * sine_part,
        ],
        axis=-1,
    )


def queries_keys(projected, positions, latent_gain, up_heads):
    head_cols = H * (DN + DR)
    row_count = projected.shape[0]
    query_cols = projected[:, :head_cols].reshape(row_count, H, DN + DR)
    query_rot = rotate(query_cols[..., DN:].astype(jnp.float32), positions).astype(jnp.bfloat16)
    latent = rms_scale(projected[:, head_cols : head_cols + LAT], latent_gain).astype(jnp.bfloat16)
    key_rot = rotate(projected[:, head_cols + LAT :].astype(jnp.float32), positions).astype(
        jnp.bfloat16
    )
    query_lat = jnp.einsum(
        "rhn,lhn->rhl", query_cols[..., :DN], up_heads[..., :DN], preferred_element_type=jnp.float32
    ).astype(jnp.bfloat16)
    queries = jnp.concatenate([query_lat, query_rot], axis=-1)
    key_rows = jnp.concatenate([latent, key_rot], axis=-1)
    return (queries, key_rows)


def prompt_attention(queries, query_ids, all_keys, all_ids, score_scale):
    row_count = queries.shape[0]
    block_rows = min(row_count, 512)
    block_count = row_count // block_rows
    query_blocks = queries.reshape(block_count, block_rows, H, queries.shape[-1])
    id_blocks = query_ids.reshape(block_count, block_rows)
    latent_keys = all_keys[:, :LAT]

    def one_block(block_args):
        query_part, id_part = block_args
        scores = (
            jnp.einsum("qhc,kc->qhk", query_part, all_keys, preferred_element_type=jnp.float32)
            * score_scale
        )
        same_prompt = id_part[:, None] // LEN == all_ids[None, :] // LEN
        allowed = same_prompt & (all_ids[None, :] <= id_part[:, None])
        scores = jnp.where(allowed[:, None, :], scores, MASKED)
        peak_score = jnp.max(scores, axis=-1, keepdims=True)
        weights = jnp.where(allowed[:, None, :], jnp.exp(scores - peak_score), 0.0)
        weight_sum = jnp.sum(weights, axis=-1, keepdims=True)
        summed = jnp.einsum(
            "qhk,kl->qhl",
            weights.astype(jnp.bfloat16),
            latent_keys,
            preferred_element_type=jnp.float32,
        )
        return (summed / weight_sum).astype(jnp.bfloat16)

    return lax.map(one_block, (query_blocks, id_blocks)).reshape(row_count, H, LAT)


def step_attention(queries, own_keys, pool, page_table, cached_lengths, score_scale):
    request_count, page_count = page_table.shape
    page_rows = pool.shape[1]
    pages = pool[page_table].reshape(request_count, page_count * page_rows, pool.shape[2])
    key_all = jnp.concatenate([pages, own_keys[:, None, :]], axis=1)
    cached_ok = (
        jnp.arange(page_count * page_rows, dtype=jnp.int32)[None, :] < cached_lengths[:, None]
    )
    allowed = jnp.concatenate([cached_ok, jnp.ones((request_count, 1), jnp.bool_)], axis=1)
    scores = (
        jnp.einsum("rhc,rkc->rhk", queries, key_all, preferred_element_type=jnp.float32)
        * score_scale
    )
    scores = jnp.where(allowed[:, None, :], scores, MASKED)
    peak_score = jnp.max(scores, axis=-1, keepdims=True)
    weights = jnp.where(allowed[:, None, :], jnp.exp(scores - peak_score), 0.0)
    weight_sum = jnp.sum(weights, axis=-1, keepdims=True)
    summed = jnp.einsum(
        "rhk,rkl->rhl",
        weights.astype(jnp.bfloat16),
        key_all[:, :, :LAT],
        preferred_element_type=jnp.float32,
    )
    return (summed / weight_sum).astype(jnp.bfloat16)


def on_device(
    prompt_rows,
    step_rows,
    attn_gain,
    latent_gain,
    joined_qkva,
    kv_up,
    out_proj,
    latent_cache,
    page_table,
    cached_lengths,
):
    prompt_count = prompt_rows.shape[0]
    mp_index = lax.axis_index("mp")
    mp_size = lax.axis_size("mp")
    score_scale = (DN + DR) ** (-0.5)
    *served, step_full, pool = gather_weights(joined_qkva, kv_up, out_proj, step_rows, latent_cache)
    stacked = jnp.concatenate([prompt_rows, step_full], axis=0)
    normed = rms_scale(stacked, attn_gain).astype(jnp.bfloat16)
    prompt_ids = jnp.arange(prompt_count, dtype=jnp.int32)
    positions = jnp.concatenate([prompt_ids % LEN, cached_lengths], axis=0)
    inputs = normed
    projected = jnp.dot(
        inputs,
        served[0],
        preferred_element_type=jnp.float32,
    )
    up_heads = served[1].reshape(LAT, H, DN + DV)
    queries, key_rows = queries_keys(
        projected.astype(jnp.bfloat16), positions, latent_gain, up_heads
    )
    prompt_queries = queries[:prompt_count]
    prompt_key_rows = key_rows[:prompt_count]
    step_queries = queries[prompt_count:]
    step_keys = key_rows[prompt_count:]
    prompt_latent = prompt_attention(
        prompt_queries, prompt_ids, prompt_key_rows, prompt_ids, score_scale
    )
    step_latent = step_attention(
        step_queries, step_keys, pool, page_table, cached_lengths, score_scale
    )
    latent_out = jnp.concatenate([prompt_latent, step_latent], axis=0)
    heads_out = jnp.einsum(
        "rhl,lhv->rhv", latent_out, up_heads[..., DN:], preferred_element_type=jnp.float32
    ).astype(jnp.bfloat16)
    heads_out = heads_out.reshape(latent_out.shape[0], H * DV)
    inputs = heads_out
    attended = jnp.dot(
        inputs,
        served[2],
        preferred_element_type=jnp.float32,
    )
    attended = attended.astype(jnp.bfloat16)
    prompt_out = attended[:prompt_count]
    col_width = attended.shape[1] // mp_size
    step_out = lax.dynamic_slice_in_dim(attended[prompt_count:], mp_index * col_width, col_width, 1)
    return (prompt_out, step_out)


def solution(mesh):
    placed = (
        P(("dp", "mp"), None),
        P("dp", "mp"),
        P(),
        P(),
        P("dp", "mp"),
        P("dp", "mp"),
        P("dp", "mp"),
        P(("dp", "mp"), None, None),
        P("dp", None),
        P("dp"),
    )
    return jax.shard_map(
        on_device,
        mesh=mesh,
        in_specs=placed,
        out_specs=(P(("dp", "mp"), None), P("dp", "mp")),
        check_vma=False,
    )
```

```python
import math

import numpy as np

import jax
import jax.numpy as jnp
from jax import lax
from jax.sharding import PartitionSpec as P

H = 16
DN = 128
DR = 64
DV = 128
LAT = 512
LEN = 512


NORM_EPS = 1e-06
ROPE_BASE = 50000.0
MASKED = -1e30


AXES = ("dp", "mp")


def _coords(i):
    dp, mp = i // 32, i % 32
    return (2 * (dp // 2) + (mp // 4) % 2, mp % 4, mp // 8, dp % 2)


def _index(x, y, z, core):
    return ((x // 2) * 2 + core) * 32 + z * 8 + (x % 2) * 4 + y


def _shift_pairs(dim, step):
    pairs = []
    for i in range(128):
        c = list(_coords(i))
        c[dim] = (c[dim] + step) % 4
        pairs.append((i, _index(*c)))
    return pairs


def torus_gather(block, cuts):
    rows = block.shape[0]
    me = lax.axis_index(AXES)
    dp, mp = me // 32, me % 32
    cx, cy, cz, ccore = 2 * (dp // 2) + (mp // 4) % 2, mp % 4, mp // 8, dp % 2
    ids = np.arange(128)
    x = 2 * (ids // 64) + (ids % 32 // 4) % 2
    y = ids % 4
    z = ids % 32 // 8
    core = (ids // 32) % 2
    rel = ((x - cx) % 4) * 16 + ((y - cy) % 4) * 4 + (z - cz) % 4
    pieces = []
    for part in range(len(cuts) - 1):
        data = block[:, cuts[part]:cuts[part + 1]]
        offs = [(0, 0, 0)]
        for stage in range(3):
            dim = (part + stage) % 3
            right = lax.ppermute(data, AXES, _shift_pairs(dim, 1))
            left = lax.ppermute(data, AXES, _shift_pairs(dim, -1))
            far = lax.ppermute(right, AXES, _shift_pairs(dim, 1))
            new_offs = list(offs)
            for delta in (-1, 1, -2):
                for o in offs:
                    o = list(o)
                    o[dim] = (o[dim] + delta) % 4
                    new_offs.append(tuple(o))
            data = jnp.concatenate([data, right, left, far], axis=0)
            offs = new_offs
        table = np.zeros((4, 4, 4), np.int32)
        for pos, o in enumerate(offs):
            table[o] = pos
        pick = jnp.take(jnp.asarray(table.reshape(-1)), rel, mode="clip") + (core - ccore) % 2 * 64
        partner = lax.ppermute(data, "dp", [(d, d ^ 1) for d in range(4)])
        slabs = jnp.concatenate([data, partner], axis=0).reshape(-1, rows, data.shape[-1])
        pieces.append(jnp.take(slabs, pick, axis=0, mode="clip"))
    return pieces


def gather_weights(joined, kv_up, out_proj, step_rows, latent_cache):
    mp_size = 32
    j = joined.astype(jnp.bfloat16).reshape(mp_size, -1)
    k = kv_up.astype(jnp.bfloat16).reshape(mp_size, -1)
    o = out_proj.astype(jnp.bfloat16).reshape(mp_size, -1)
    cache = jnp.broadcast_to(latent_cache.reshape(1, -1), (mp_size, latent_cache.size))
    packed = jnp.concatenate([j, k, o, cache], axis=1)
    swapped = lax.all_to_all(packed, "mp", 0, 0, tiled=True)
    jw, kw = j.shape[1], k.shape[1]
    jr = swapped[:, :jw].reshape(mp_size, 16, 114).transpose(1, 0, 2).reshape(16, mp_size * 114)
    kr = swapped[:, jw:jw + kw].reshape(mp_size, 4, 128).transpose(1, 0, 2).reshape(16, 1024)
    ow = o.shape[1]
    pool = swapped[:, jw + kw + ow:].reshape((mp_size * latent_cache.shape[0],) + latent_cache.shape[1:])
    orr = swapped[:, jw + kw:jw + kw + ow].reshape(mp_size, 16, 64).transpose(1, 0, 2).reshape(16, mp_size * 64)
    jr = jnp.pad(jr, ((0, 0), (0, 3712 - 3648)))
    step_count, step_width = step_rows.shape
    step_block = jnp.pad(step_rows, ((0, 16 - step_count), (0, 128 - step_width)))
    block = jnp.concatenate([jr, orr, kr, step_block], axis=1)
    first, second, third = torus_gather(block, [0, 2304, 4608, 6912])
    w1 = (first.reshape(2048, 2304), second[:, :, :1344].reshape(2048, 1344))
    w3 = (second[:, :, 1408:].reshape(2048, 896), third[:, :, :1152].reshape(2048, 1152))
    w2 = third[:, :, 1152:2176].reshape(128, 4, 4096).reshape(512, 4096)
    steps = lax.dynamic_slice_in_dim(third[:, :step_count, 2176:2176 + step_width], lax.axis_index("dp") * mp_size, mp_size, 0)
    steps = steps.transpose(1, 0, 2).reshape(step_count, mp_size * step_width)
    return w1, w2, w3, steps, pool


def rms_scale(values, scales):
    widened = values.astype(jnp.float32)
    mean_square = jnp.mean(widened * widened, axis=-1, keepdims=True)
    return widened * lax.rsqrt(mean_square + NORM_EPS) * scales


def rotate(values, positions):
    rot_width = values.shape[-1]
    half_width = rot_width // 2
    freq_steps = jnp.arange(half_width, dtype=jnp.float32)
    inv_freqs = jnp.exp(freq_steps * (-2.0 * math.log(ROPE_BASE) / rot_width))
    angles = positions.astype(jnp.float32)[:, None] * inv_freqs[None, :]
    angle_shape = (positions.shape[0],) + (1,) * (values.ndim - 2) + (half_width,)
    cosine = jnp.cos(angles).reshape(angle_shape)
    sine_part = jnp.sin(angles).reshape(angle_shape)
    lower_half = values[..., :half_width]
    upper_half = values[..., half_width:]
    return jnp.concatenate(
        [
            lower_half * cosine - upper_half * sine_part,
            upper_half * cosine + lower_half * sine_part,
        ],
        axis=-1,
    )


def queries_keys(projected, positions, latent_gain, up_heads):
    head_cols = H * (DN + DR)
    row_count = projected.shape[0]
    query_cols = projected[:, :head_cols].reshape(row_count, H, DN + DR)
    query_rot = rotate(query_cols[..., DN:].astype(jnp.float32), positions).astype(jnp.bfloat16)
    latent = rms_scale(projected[:, head_cols : head_cols + LAT], latent_gain).astype(jnp.bfloat16)
    key_rot = rotate(projected[:, head_cols + LAT :].astype(jnp.float32), positions).astype(
        jnp.bfloat16
    )
    query_lat = jnp.einsum(
        "rhn,lhn->rhl", query_cols[..., :DN], up_heads[..., :DN], preferred_element_type=jnp.float32
    ).astype(jnp.bfloat16)
    queries = jnp.concatenate([query_lat, query_rot], axis=-1)
    key_rows = jnp.concatenate([latent, key_rot], axis=-1)
    return (queries, key_rows)


def prompt_attention(queries, query_ids, all_keys, all_ids, score_scale):
    row_count = queries.shape[0]
    block_rows = min(row_count, 512)
    block_count = row_count // block_rows
    query_blocks = queries.reshape(block_count, block_rows, H, queries.shape[-1])
    id_blocks = query_ids.reshape(block_count, block_rows)
    latent_keys = all_keys[:, :LAT]

    def one_block(block_args):
        query_part, id_part = block_args
        scores = (
            jnp.einsum("qhc,kc->qhk", query_part, all_keys, preferred_element_type=jnp.float32)
            * score_scale
        )
        same_prompt = id_part[:, None] // LEN == all_ids[None, :] // LEN
        allowed = same_prompt & (all_ids[None, :] <= id_part[:, None])
        scores = jnp.where(allowed[:, None, :], scores, MASKED)
        peak_score = jnp.max(scores, axis=-1, keepdims=True)
        weights = jnp.where(allowed[:, None, :], jnp.exp(scores - peak_score), 0.0)
        weight_sum = jnp.sum(weights, axis=-1, keepdims=True)
        summed = jnp.einsum(
            "qhk,kl->qhl",
            weights.astype(jnp.bfloat16),
            latent_keys,
            preferred_element_type=jnp.float32,
        )
        return (summed / weight_sum).astype(jnp.bfloat16)

    return lax.map(one_block, (query_blocks, id_blocks)).reshape(row_count, H, LAT)


def step_attention(queries, own_keys, pool, page_table, cached_lengths, score_scale):
    request_count, page_count = page_table.shape
    page_rows = pool.shape[1]
    pages = pool[page_table].reshape(request_count, page_count * page_rows, pool.shape[2])
    key_all = jnp.concatenate([pages, own_keys[:, None, :]], axis=1)
    cached_ok = (
        jnp.arange(page_count * page_rows, dtype=jnp.int32)[None, :] < cached_lengths[:, None]
    )
    allowed = jnp.concatenate([cached_ok, jnp.ones((request_count, 1), jnp.bool_)], axis=1)
    scores = (
        jnp.einsum("rhc,rkc->rhk", queries, key_all, preferred_element_type=jnp.float32)
        * score_scale
    )
    scores = jnp.where(allowed[:, None, :], scores, MASKED)
    peak_score = jnp.max(scores, axis=-1, keepdims=True)
    weights = jnp.where(allowed[:, None, :], jnp.exp(scores - peak_score), 0.0)
    weight_sum = jnp.sum(weights, axis=-1, keepdims=True)
    summed = jnp.einsum(
        "rhk,rkl->rhl",
        weights.astype(jnp.bfloat16),
        key_all[:, :, :LAT],
        preferred_element_type=jnp.float32,
    )
    return (summed / weight_sum).astype(jnp.bfloat16)


def on_device(
    prompt_rows,
    step_rows,
    attn_gain,
    latent_gain,
    joined_qkva,
    kv_up,
    out_proj,
    latent_cache,
    page_table,
    cached_lengths,
):
    prompt_count = prompt_rows.shape[0]
    mp_index = lax.axis_index("mp")
    mp_size = lax.axis_size("mp")
    score_scale = (DN + DR) ** (-0.5)
    *served, step_full, pool = gather_weights(joined_qkva, kv_up, out_proj, step_rows, latent_cache)
    stacked = jnp.concatenate([prompt_rows, step_full], axis=0)
    normed = rms_scale(stacked, attn_gain).astype(jnp.bfloat16)
    prompt_ids = jnp.arange(prompt_count, dtype=jnp.int32)
    positions = jnp.concatenate([prompt_ids % LEN, cached_lengths], axis=0)
    inputs = normed
    projected = jnp.concatenate(
        [jnp.dot(inputs, piece, preferred_element_type=jnp.float32) for piece in served[0]], axis=1
    )
    up_heads = served[1].reshape(LAT, H, DN + DV)
    queries, key_rows = queries_keys(
        projected.astype(jnp.bfloat16), positions, latent_gain, up_heads
    )
    prompt_queries = queries[:prompt_count]
    prompt_key_rows = key_rows[:prompt_count]
    step_queries = queries[prompt_count:]
    step_keys = key_rows[prompt_count:]
    prompt_latent = prompt_attention(
        prompt_queries, prompt_ids, prompt_key_rows, prompt_ids, score_scale
    )
    step_latent = step_attention(
        step_queries, step_keys, pool, page_table, cached_lengths, score_scale
    )
    latent_out = jnp.concatenate([prompt_latent, step_latent], axis=0)
    heads_out = jnp.einsum(
        "rhl,lhv->rhv", latent_out, up_heads[..., DN:], preferred_element_type=jnp.float32
    ).astype(jnp.bfloat16)
    heads_out = heads_out.reshape(latent_out.shape[0], H * DV)
    inputs = heads_out
    attended = jnp.concatenate(
        [jnp.dot(inputs, piece, preferred_element_type=jnp.float32) for piece in served[2]], axis=1
    )
    attended = attended.astype(jnp.bfloat16)
    prompt_out = attended[:prompt_count]
    col_width = attended.shape[1] // mp_size
    step_out = lax.dynamic_slice_in_dim(attended[prompt_count:], mp_index * col_width, col_width, 1)
    return (prompt_out, step_out)


def solution(mesh):
    placed = (
        P(("dp", "mp"), None),
        P("dp", "mp"),
        P(),
        P(),
        P("dp", "mp"),
        P("dp", "mp"),
        P("dp", "mp"),
        P(("dp", "mp"), None, None),
        P("dp", None),
        P("dp"),
    )
    return jax.shard_map(
        on_device,
        mesh=mesh,
        in_specs=placed,
        out_specs=(P(("dp", "mp"), None), P("dp", "mp")),
        check_vma=False,
    )
```

```python
import math

import numpy as np

import jax
import jax.numpy as jnp
from jax import lax
from jax.sharding import PartitionSpec as P

H = 16
DN = 128
DR = 64
DV = 128
LAT = 512
LEN = 512


NORM_EPS = 1e-06
ROPE_BASE = 50000.0
MASKED = -1e30


AXES = ("dp", "mp")


def _coords(i):
    dp, mp = i // 32, i % 32
    return (2 * (dp // 2) + (mp // 4) % 2, mp % 4, mp // 8, dp % 2)


def _index(x, y, z, core):
    return ((x // 2) * 2 + core) * 32 + z * 8 + (x % 2) * 4 + y


def _shift_pairs(dim, step):
    pairs = []
    for i in range(128):
        c = list(_coords(i))
        c[dim] = (c[dim] + step) % 4
        pairs.append((i, _index(*c)))
    return pairs


def torus_gather(block, cuts):
    rows = block.shape[0]
    me = lax.axis_index(AXES)
    dp, mp = me // 32, me % 32
    cx, cy, cz, ccore = 2 * (dp // 2) + (mp // 4) % 2, mp % 4, mp // 8, dp % 2
    ids = np.arange(128)
    x = 2 * (ids // 64) + (ids % 32 // 4) % 2
    y = ids % 4
    z = ids % 32 // 8
    core = (ids // 32) % 2
    rel = ((x - cx) % 4) * 16 + ((y - cy) % 4) * 4 + (z - cz) % 4
    pieces = []
    for part in range(len(cuts) - 1):
        data = block[:, cuts[part]:cuts[part + 1]]
        offs = [(0, 0, 0)]
        for stage in range(3):
            dim = (part + stage) % 3
            right = lax.ppermute(data, AXES, _shift_pairs(dim, 1))
            left = lax.ppermute(data, AXES, _shift_pairs(dim, -1))
            far = lax.ppermute(right, AXES, _shift_pairs(dim, 1))
            new_offs = list(offs)
            for delta in (-1, 1, -2):
                for o in offs:
                    o = list(o)
                    o[dim] = (o[dim] + delta) % 4
                    new_offs.append(tuple(o))
            data = jnp.concatenate([data, right, left, far], axis=0)
            offs = new_offs
        table = np.zeros((4, 4, 4), np.int32)
        for pos, o in enumerate(offs):
            table[o] = pos
        pick = jnp.take(jnp.asarray(table.reshape(-1)), rel, mode="clip") + (core - ccore) % 2 * 64
        partner = lax.ppermute(data, "dp", [(d, d ^ 1) for d in range(4)])
        slabs = jnp.concatenate([data, partner], axis=0).reshape(-1, rows, data.shape[-1])
        pieces.append(jnp.take(slabs, pick, axis=0, mode="clip"))
    return jnp.concatenate(pieces, axis=2)


def gather_weights(joined, kv_up, out_proj, step_rows, latent_cache):
    mp_size = 32
    j = joined.astype(jnp.bfloat16).reshape(mp_size, -1)
    k = kv_up.astype(jnp.bfloat16).reshape(mp_size, -1)
    o = out_proj.astype(jnp.bfloat16).reshape(mp_size, -1)
    cache = jnp.broadcast_to(latent_cache.reshape(1, -1), (mp_size, latent_cache.size))
    packed = jnp.concatenate([j, k, o, cache], axis=1)
    packed = jnp.pad(packed, ((0, 0), (0, -packed.shape[1] % 256)))
    swapped = lax.all_to_all(packed, "mp", 0, 0, tiled=True)
    jw, kw = j.shape[1], k.shape[1]
    jr = swapped[:, :jw].reshape(mp_size, 16, 114).transpose(1, 0, 2).reshape(16, mp_size * 114)
    kr = swapped[:, jw:jw + kw].reshape(mp_size // 2, 2, 4, 128).transpose(2, 1, 0, 3).reshape(16, 1024)
    ow = o.shape[1]
    pool = swapped[:, jw + kw + ow:jw + kw + ow + latent_cache.size].reshape((mp_size * latent_cache.shape[0],) + latent_cache.shape[1:])
    orr = swapped[:, jw + kw:jw + kw + ow].reshape(mp_size, 16, 64).transpose(1, 0, 2).reshape(16, mp_size * 64)
    jr = jnp.pad(jr, ((0, 0), (0, 3712 - 3648)))
    step_count, step_width = step_rows.shape
    step_block = jnp.pad(step_rows, ((0, 16 - step_count), (0, 128 - step_width)))
    block = jnp.concatenate([jr, orr, kr, step_block], axis=1)
    g = torus_gather(block, [0, 2304, 4608, 6912])
    w1 = g[:, :, :3648].reshape(2048, 3648)
    w3 = g[:, :, 3712:5760].reshape(2048, 2048)
    w2 = g[:, :, 5760:6784].reshape(128, 4, 4096).reshape(512, 4096)
    steps = lax.dynamic_slice_in_dim(g[:, :step_count, 6784:6784 + step_width], lax.axis_index("dp") * mp_size, mp_size, 0)
    steps = steps.transpose(1, 0, 2).reshape(step_count, mp_size * step_width)
    return w1, w2, w3, steps, pool


def rms_scale(values, scales):
    widened = values.astype(jnp.float32)
    mean_square = jnp.mean(widened * widened, axis=-1, keepdims=True)
    return widened * lax.rsqrt(mean_square + NORM_EPS) * scales


def rotate(values, positions):
    rot_width = values.shape[-1]
    half_width = rot_width // 2
    freq_steps = jnp.arange(half_width, dtype=jnp.float32)
    inv_freqs = jnp.exp(freq_steps * (-2.0 * math.log(ROPE_BASE) / rot_width))
    angles = positions.astype(jnp.float32)[:, None] * inv_freqs[None, :]
    angle_shape = (positions.shape[0],) + (1,) * (values.ndim - 2) + (half_width,)
    cosine = jnp.cos(angles).reshape(angle_shape)
    sine_part = jnp.sin(angles).reshape(angle_shape)
    lower_half = values[..., :half_width]
    upper_half = values[..., half_width:]
    return jnp.concatenate(
        [
            lower_half * cosine - upper_half * sine_part,
            upper_half * cosine + lower_half * sine_part,
        ],
        axis=-1,
    )


def queries_keys(projected, positions, latent_gain, up_heads):
    head_cols = H * (DN + DR)
    row_count = projected.shape[0]
    query_cols = projected[:, :head_cols].reshape(row_count, H, DN + DR)
    query_rot = rotate(query_cols[..., DN:].astype(jnp.float32), positions).astype(jnp.bfloat16)
    latent = rms_scale(projected[:, head_cols : head_cols + LAT], latent_gain).astype(jnp.bfloat16)
    key_rot = rotate(projected[:, head_cols + LAT :].astype(jnp.float32), positions).astype(
        jnp.bfloat16
    )
    query_lat = jnp.einsum(
        "rhn,lhn->rhl", query_cols[..., :DN], up_heads[:, 0], preferred_element_type=jnp.float32
    ).astype(jnp.bfloat16)
    queries = jnp.concatenate([query_lat, query_rot], axis=-1)
    key_rows = jnp.concatenate([latent, key_rot], axis=-1)
    return (queries, key_rows)


def prompt_attention(queries, query_ids, all_keys, all_ids, score_scale):
    row_count = queries.shape[0]
    block_rows = min(row_count, 512)
    block_count = row_count // block_rows
    query_blocks = queries.reshape(block_count, block_rows, H, queries.shape[-1])
    id_blocks = query_ids.reshape(block_count, block_rows)
    latent_keys = all_keys[:, :LAT]

    def one_block(block_args):
        query_part, id_part = block_args
        scores = (
            jnp.einsum("qhc,kc->qhk", query_part, all_keys, preferred_element_type=jnp.float32)
            * score_scale
        )
        same_prompt = id_part[:, None] // LEN == all_ids[None, :] // LEN
        allowed = same_prompt & (all_ids[None, :] <= id_part[:, None])
        scores = jnp.where(allowed[:, None, :], scores, MASKED)
        peak_score = jnp.max(scores, axis=-1, keepdims=True)
        weights = jnp.where(allowed[:, None, :], jnp.exp(scores - peak_score), 0.0)
        weight_sum = jnp.sum(weights, axis=-1, keepdims=True)
        summed = jnp.einsum(
            "qhk,kl->qhl",
            weights.astype(jnp.bfloat16),
            latent_keys,
            preferred_element_type=jnp.float32,
        )
        return (summed / weight_sum).astype(jnp.bfloat16)

    return lax.map(one_block, (query_blocks, id_blocks)).reshape(row_count, H, LAT)


def step_attention(queries, own_keys, pool, page_table, cached_lengths, score_scale):
    request_count, page_count = page_table.shape
    page_rows = pool.shape[1]
    pages = pool[page_table].reshape(request_count, page_count * page_rows, pool.shape[2])
    key_all = jnp.concatenate([pages, own_keys[:, None, :]], axis=1)
    cached_ok = (
        jnp.arange(page_count * page_rows, dtype=jnp.int32)[None, :] < cached_lengths[:, None]
    )
    allowed = jnp.concatenate([cached_ok, jnp.ones((request_count, 1), jnp.bool_)], axis=1)
    scores = (
        jnp.einsum("rhc,rkc->rhk", queries, key_all, preferred_element_type=jnp.float32)
        * score_scale
    )
    scores = jnp.where(allowed[:, None, :], scores, MASKED)
    peak_score = jnp.max(scores, axis=-1, keepdims=True)
    weights = jnp.where(allowed[:, None, :], jnp.exp(scores - peak_score), 0.0)
    weight_sum = jnp.sum(weights, axis=-1, keepdims=True)
    summed = jnp.einsum(
        "rhk,rkl->rhl",
        weights.astype(jnp.bfloat16),
        key_all[:, :, :LAT],
        preferred_element_type=jnp.float32,
    )
    return (summed / weight_sum).astype(jnp.bfloat16)


def on_device(
    prompt_rows,
    step_rows,
    attn_gain,
    latent_gain,
    joined_qkva,
    kv_up,
    out_proj,
    latent_cache,
    page_table,
    cached_lengths,
):
    prompt_count = prompt_rows.shape[0]
    mp_index = lax.axis_index("mp")
    mp_size = lax.axis_size("mp")
    score_scale = (DN + DR) ** (-0.5)
    *served, step_full, pool = gather_weights(joined_qkva, kv_up, out_proj, step_rows, latent_cache)
    stacked = jnp.concatenate([prompt_rows, step_full], axis=0)
    normed = rms_scale(stacked, attn_gain).astype(jnp.bfloat16)
    prompt_ids = jnp.arange(prompt_count, dtype=jnp.int32)
    positions = jnp.concatenate([prompt_ids % LEN, cached_lengths], axis=0)
    inputs = normed
    projected = jnp.dot(
        inputs,
        served[0],
        preferred_element_type=jnp.float32,
    )
    up_heads = served[1].reshape(LAT, 2, H, DN)
    queries, key_rows = queries_keys(
        projected.astype(jnp.bfloat16), positions, latent_gain, up_heads
    )
    prompt_queries = queries[:prompt_count]
    prompt_key_rows = key_rows[:prompt_count]
    step_queries = queries[prompt_count:]
    step_keys = key_rows[prompt_count:]
    prompt_latent = prompt_attention(
        prompt_queries, prompt_ids, prompt_key_rows, prompt_ids, score_scale
    )
    step_latent = step_attention(
        step_queries, step_keys, pool, page_table, cached_lengths, score_scale
    )
    latent_out = jnp.concatenate([prompt_latent, step_latent], axis=0)
    heads_out = jnp.einsum(
        "rhl,lhv->rhv", latent_out, up_heads[:, 1], preferred_element_type=jnp.float32
    ).astype(jnp.bfloat16)
    heads_out = heads_out.reshape(latent_out.shape[0], H * DV)
    inputs = heads_out
    attended = jnp.dot(
        inputs,
        served[2],
        preferred_element_type=jnp.float32,
    )
    attended = attended.astype(jnp.bfloat16)
    prompt_out = attended[:prompt_count]
    col_width = attended.shape[1] // mp_size
    step_out = lax.dynamic_slice_in_dim(attended[prompt_count:], mp_index * col_width, col_width, 1)
    return (prompt_out, step_out)


def solution(mesh):
    placed = (
        P(("dp", "mp"), None),
        P("dp", "mp"),
        P(),
        P(),
        P("dp", "mp"),
        P("dp", "mp"),
        P("dp", "mp"),
        P(("dp", "mp"), None, None),
        P("dp", None),
        P("dp"),
    )
    return jax.shard_map(
        on_device,
        mesh=mesh,
        in_specs=placed,
        out_specs=(P(("dp", "mp"), None), P("dp", "mp")),
        check_vma=False,
    )
```

```python
import math

import numpy as np

import jax
import jax.numpy as jnp
from jax import lax
from jax.sharding import PartitionSpec as P

H = 16
DN = 128
DR = 64
DV = 128
LAT = 512
LEN = 512


NORM_EPS = 1e-06
ROPE_BASE = 50000.0
MASKED = -1e30


AXES = ("dp", "mp")


def _coords(i):
    dp, mp = i // 32, i % 32
    return (2 * (dp // 2) + (mp // 4) % 2, mp % 4, mp // 8, dp % 2)


def _index(x, y, z, core):
    return ((x // 2) * 2 + core) * 32 + z * 8 + (x % 2) * 4 + y


def _shift_pairs(dim, step):
    pairs = []
    for i in range(128):
        c = list(_coords(i))
        c[dim] = (c[dim] + step) % 4
        pairs.append((i, _index(*c)))
    return pairs


def torus_gather(block, cuts):
    rows = block.shape[0]
    me = lax.axis_index(AXES)
    dp, mp = me // 32, me % 32
    cx, cy, cz, ccore = 2 * (dp // 2) + (mp // 4) % 2, mp % 4, mp // 8, dp % 2
    ids = np.arange(128)
    x = 2 * (ids // 64) + (ids % 32 // 4) % 2
    y = ids % 4
    z = ids % 32 // 8
    core = (ids // 32) % 2
    rel = ((x - cx) % 4) * 16 + ((y - cy) % 4) * 4 + (z - cz) % 4
    pieces = []
    for part in range(len(cuts) - 1):
        data = block[:, cuts[part]:cuts[part + 1]]
        offs = [(0, 0, 0)]
        for stage in range(3):
            dim = (part + stage) % 3
            right = lax.ppermute(data, AXES, _shift_pairs(dim, 1))
            left = lax.ppermute(data, AXES, _shift_pairs(dim, -1))
            far = lax.ppermute(right, AXES, _shift_pairs(dim, 1))
            new_offs = list(offs)
            for delta in (-1, 1, -2):
                for o in offs:
                    o = list(o)
                    o[dim] = (o[dim] + delta) % 4
                    new_offs.append(tuple(o))
            data = jnp.concatenate([data, right, left, far], axis=0)
            offs = new_offs
        table = np.zeros((4, 4, 4), np.int32)
        for pos, o in enumerate(offs):
            table[o] = pos
        pick = jnp.take(jnp.asarray(table.reshape(-1)), rel, mode="clip") + (core - ccore) % 2 * 64
        partner = lax.ppermute(data, "dp", [(d, d ^ 1) for d in range(4)])
        slabs = jnp.concatenate([data, partner], axis=0).reshape(-1, rows, data.shape[-1])
        pieces.append(jnp.take(slabs, pick, axis=0, mode="clip"))
    return jnp.concatenate(pieces, axis=2)


def gather_weights(joined, kv_up, out_proj, step_rows, latent_cache):
    mp_size = 32
    j = joined.astype(jnp.bfloat16).reshape(mp_size, -1)
    k = kv_up.astype(jnp.bfloat16).reshape(mp_size, -1)
    o = out_proj.astype(jnp.bfloat16).reshape(mp_size, -1)
    cache = jnp.broadcast_to(latent_cache.reshape(1, -1), (mp_size, latent_cache.size))
    packed = jnp.concatenate([j, k, o, cache], axis=1)
    packed = jnp.pad(packed, ((0, 0), (0, -packed.shape[1] % 256)))
    swapped = lax.all_to_all(packed, "mp", 0, 0, tiled=True)
    jw, kw = j.shape[1], k.shape[1]
    jr = swapped[:, :jw].reshape(mp_size, 16, 114).transpose(1, 0, 2).reshape(16, mp_size * 114)
    kr = swapped[:, jw:jw + kw].reshape(mp_size // 2, 2, 4, 128).transpose(2, 1, 0, 3).reshape(16, 1024)
    ow = o.shape[1]
    pool = swapped[:, jw + kw + ow:jw + kw + ow + latent_cache.size].reshape((mp_size * latent_cache.shape[0],) + latent_cache.shape[1:])
    orr = swapped[:, jw + kw:jw + kw + ow].reshape(mp_size, 16, 64).transpose(1, 0, 2).reshape(16, mp_size * 64)
    jr = jnp.pad(jr, ((0, 0), (0, 3712 - 3648)))
    step_count, step_width = step_rows.shape
    step_block = jnp.pad(step_rows, ((0, 16 - step_count), (0, 128 - step_width)))
    block = jnp.concatenate([jr, orr, kr, step_block], axis=1)
    g = torus_gather(block, [0, 2304, 4608, 6912])
    w1 = g[:, :, :3648].reshape(2048, 3648)
    w3 = g[:, :, 3712:5760].reshape(2048, 2048)
    w2 = g[:, :, 5760:6784].reshape(128, 4, 4096).reshape(512, 4096)
    steps = lax.dynamic_slice_in_dim(g[:, :step_count, 6784:6784 + step_width], lax.axis_index("dp") * mp_size, mp_size, 0)
    steps = steps.transpose(1, 0, 2).reshape(step_count, mp_size * step_width)
    return w1, w2, w3, steps, pool


def rms_scale(values, scales):
    widened = values.astype(jnp.float32)
    mean_square = jnp.mean(widened * widened, axis=-1, keepdims=True)
    return widened * lax.rsqrt(mean_square + NORM_EPS) * scales


def rotate(values, positions):
    rot_width = values.shape[-1]
    half_width = rot_width // 2
    freq_steps = jnp.arange(half_width, dtype=jnp.float32)
    inv_freqs = jnp.exp(freq_steps * (-2.0 * math.log(ROPE_BASE) / rot_width))
    angles = positions.astype(jnp.float32)[:, None] * inv_freqs[None, :]
    angle_shape = (positions.shape[0],) + (1,) * (values.ndim - 2) + (half_width,)
    cosine = jnp.cos(angles).reshape(angle_shape)
    sine_part = jnp.sin(angles).reshape(angle_shape)
    lower_half = values[..., :half_width]
    upper_half = values[..., half_width:]
    return jnp.concatenate(
        [
            lower_half * cosine - upper_half * sine_part,
            upper_half * cosine + lower_half * sine_part,
        ],
        axis=-1,
    )


def queries_keys(projected, positions, latent_gain, up_heads):
    head_cols = H * (DN + DR)
    row_count = projected.shape[0]
    query_cols = projected[:, :head_cols].reshape(row_count, H, DN + DR)
    query_rot = rotate(query_cols[..., DN:].astype(jnp.float32), positions).astype(jnp.bfloat16)
    latent = rms_scale(projected[:, head_cols : head_cols + LAT], latent_gain).astype(jnp.bfloat16)
    key_rot = rotate(projected[:, head_cols + LAT :].astype(jnp.float32), positions).astype(
        jnp.bfloat16
    )
    query_lat = jnp.einsum(
        "rhn,lhn->rhl", query_cols[..., :DN], up_heads[:, 0], preferred_element_type=jnp.float32
    ).astype(jnp.bfloat16)
    queries = jnp.concatenate([query_lat, query_rot], axis=-1)
    key_rows = jnp.concatenate([latent, key_rot], axis=-1)
    return (queries, key_rows)


def prompt_attention(queries, query_ids, all_keys, all_ids, score_scale):
    row_count = queries.shape[0]
    block_rows = min(row_count, LEN // 2)
    outputs = []
    for start in range(0, row_count, block_rows):
        stop = start + block_rows
        key_start = start - start % LEN
        query_part, id_part = queries[start:stop], query_ids[start:stop]
        key_part, key_ids = all_keys[key_start:stop], all_ids[key_start:stop]
        scores = (
            jnp.einsum("qhc,kc->qhk", query_part, key_part, preferred_element_type=jnp.float32)
            * score_scale
        )
        allowed = key_ids[None, :] <= id_part[:, None]
        scores = jnp.where(allowed[:, None, :], scores, MASKED)
        peak_score = jnp.max(scores, axis=-1, keepdims=True)
        weights = jnp.where(allowed[:, None, :], jnp.exp(scores - peak_score), 0.0)
        weight_sum = jnp.sum(weights, axis=-1, keepdims=True)
        summed = jnp.einsum(
            "qhk,kl->qhl",
            weights.astype(jnp.bfloat16),
            key_part[:, :LAT],
            preferred_element_type=jnp.float32,
        )
        outputs.append((summed / weight_sum).astype(jnp.bfloat16))
    return jnp.concatenate(outputs, axis=0)


def step_attention(queries, own_keys, pool, page_table, cached_lengths, score_scale):
    request_count, page_count = page_table.shape
    page_rows = pool.shape[1]
    pages = pool[page_table].reshape(request_count, page_count * page_rows, pool.shape[2])
    key_all = jnp.concatenate([pages, own_keys[:, None, :]], axis=1)
    cached_ok = (
        jnp.arange(page_count * page_rows, dtype=jnp.int32)[None, :] < cached_lengths[:, None]
    )
    allowed = jnp.concatenate([cached_ok, jnp.ones((request_count, 1), jnp.bool_)], axis=1)
    scores = (
        jnp.einsum("rhc,rkc->rhk", queries, key_all, preferred_element_type=jnp.float32)
        * score_scale
    )
    scores = jnp.where(allowed[:, None, :], scores, MASKED)
    peak_score = jnp.max(scores, axis=-1, keepdims=True)
    weights = jnp.where(allowed[:, None, :], jnp.exp(scores - peak_score), 0.0)
    weight_sum = jnp.sum(weights, axis=-1, keepdims=True)
    summed = jnp.einsum(
        "rhk,rkl->rhl",
        weights.astype(jnp.bfloat16),
        key_all[:, :, :LAT],
        preferred_element_type=jnp.float32,
    )
    return (summed / weight_sum).astype(jnp.bfloat16)


def on_device(
    prompt_rows,
    step_rows,
    attn_gain,
    latent_gain,
    joined_qkva,
    kv_up,
    out_proj,
    latent_cache,
    page_table,
    cached_lengths,
):
    prompt_count = prompt_rows.shape[0]
    mp_index = lax.axis_index("mp")
    mp_size = lax.axis_size("mp")
    score_scale = (DN + DR) ** (-0.5)
    *served, step_full, pool = gather_weights(joined_qkva, kv_up, out_proj, step_rows, latent_cache)
    stacked = jnp.concatenate([prompt_rows, step_full], axis=0)
    normed = rms_scale(stacked, attn_gain).astype(jnp.bfloat16)
    prompt_ids = jnp.arange(prompt_count, dtype=jnp.int32)
    positions = jnp.concatenate([prompt_ids % LEN, cached_lengths], axis=0)
    inputs = normed
    projected = jnp.dot(
        inputs,
        served[0],
        preferred_element_type=jnp.float32,
    )
    up_heads = served[1].reshape(LAT, 2, H, DN)
    queries, key_rows = queries_keys(
        projected.astype(jnp.bfloat16), positions, latent_gain, up_heads
    )
    prompt_queries = queries[:prompt_count]
    prompt_key_rows = key_rows[:prompt_count]
    step_queries = queries[prompt_count:]
    step_keys = key_rows[prompt_count:]
    prompt_latent = prompt_attention(
        prompt_queries, prompt_ids, prompt_key_rows, prompt_ids, score_scale
    )
    step_latent = step_attention(
        step_queries, step_keys, pool, page_table, cached_lengths, score_scale
    )
    latent_out = jnp.concatenate([prompt_latent, step_latent], axis=0)
    heads_out = jnp.einsum(
        "rhl,lhv->rhv", latent_out, up_heads[:, 1], preferred_element_type=jnp.float32
    ).astype(jnp.bfloat16)
    heads_out = heads_out.reshape(latent_out.shape[0], H * DV)
    inputs = heads_out
    attended = jnp.dot(
        inputs,
        served[2],
        preferred_element_type=jnp.float32,
    )
    attended = attended.astype(jnp.bfloat16)
    prompt_out = attended[:prompt_count]
    col_width = attended.shape[1] // mp_size
    step_out = lax.dynamic_slice_in_dim(attended[prompt_count:], mp_index * col_width, col_width, 1)
    return (prompt_out, step_out)


def solution(mesh):
    placed = (
        P(("dp", "mp"), None),
        P("dp", "mp"),
        P(),
        P(),
        P("dp", "mp"),
        P("dp", "mp"),
        P("dp", "mp"),
        P(("dp", "mp"), None, None),
        P("dp", None),
        P("dp"),
    )
    return jax.shard_map(
        on_device,
        mesh=mesh,
        in_specs=placed,
        out_specs=(P(("dp", "mp"), None), P("dp", "mp")),
        check_vma=False,
    )
```

```python
import math

import numpy as np

import jax
import jax.numpy as jnp
from jax import lax
from jax.sharding import PartitionSpec as P

H = 16
DN = 128
DR = 64
DV = 128
LAT = 512
LEN = 512


NORM_EPS = 1e-06
ROPE_BASE = 50000.0
MASKED = -1e30


AXES = ("dp", "mp")


def _coords(i):
    dp, mp = i // 32, i % 32
    return (2 * (dp // 2) + (mp // 4) % 2, mp % 4, mp // 8, dp % 2)


def _index(x, y, z, core):
    return ((x // 2) * 2 + core) * 32 + z * 8 + (x % 2) * 4 + y


def _shift_pairs(dim, step):
    pairs = []
    for i in range(128):
        c = list(_coords(i))
        c[dim] = (c[dim] + step) % 4
        pairs.append((i, _index(*c)))
    return pairs


def torus_gather(block, cuts):
    rows = block.shape[0]
    me = lax.axis_index(AXES)
    dp, mp = me // 32, me % 32
    cx, cy, cz, ccore = 2 * (dp // 2) + (mp // 4) % 2, mp % 4, mp // 8, dp % 2
    ids = np.arange(128)
    x = 2 * (ids // 64) + (ids % 32 // 4) % 2
    y = ids % 4
    z = ids % 32 // 8
    core = (ids // 32) % 2
    rel = ((x - cx) % 4) * 16 + ((y - cy) % 4) * 4 + (z - cz) % 4
    pieces = []
    for part in range(len(cuts) - 1):
        data = block[:, cuts[part]:cuts[part + 1]]
        offs = [(0, 0, 0)]
        for stage in range(3):
            dim = (part + stage) % 3
            right = lax.ppermute(data, AXES, _shift_pairs(dim, 1))
            left = lax.ppermute(data, AXES, _shift_pairs(dim, -1))
            far = lax.ppermute(right, AXES, _shift_pairs(dim, 1))
            new_offs = list(offs)
            for delta in (-1, 1, -2):
                for o in offs:
                    o = list(o)
                    o[dim] = (o[dim] + delta) % 4
                    new_offs.append(tuple(o))
            data = jnp.concatenate([data, right, left, far], axis=0)
            offs = new_offs
        table = np.zeros((4, 4, 4), np.int32)
        for pos, o in enumerate(offs):
            table[o] = pos
        pick = jnp.take(jnp.asarray(table.reshape(-1)), rel, mode="clip") + (core - ccore) % 2 * 64
        partner = lax.ppermute(data, "dp", [(d, d ^ 1) for d in range(4)])
        slabs = jnp.concatenate([data, partner], axis=0).reshape(-1, rows, data.shape[-1])
        pieces.append(jnp.take(slabs, pick, axis=0, mode="clip"))
    return jnp.concatenate(pieces, axis=2)


def gather_weights(joined, kv_up, out_proj, step_rows, latent_cache):
    mp_size = 32
    j = joined.astype(jnp.bfloat16).reshape(mp_size, -1)
    k = kv_up.astype(jnp.bfloat16).reshape(mp_size, -1)
    o = out_proj.astype(jnp.bfloat16).reshape(mp_size, -1)
    cache = jnp.broadcast_to(latent_cache.reshape(1, -1), (mp_size, latent_cache.size))
    packed = jnp.concatenate([j, k, o, cache], axis=1)
    packed = jnp.pad(packed, ((0, 0), (0, -packed.shape[1] % 256)))
    swapped = lax.all_to_all(packed, "mp", 0, 0, tiled=True)
    jw, kw = j.shape[1], k.shape[1]
    jr = swapped[:, :jw].reshape(mp_size, 16, 114).transpose(1, 0, 2).reshape(16, mp_size * 114)
    kr = swapped[:, jw:jw + kw].reshape(mp_size // 2, 2, 4, 128).transpose(2, 1, 0, 3).reshape(16, 1024)
    ow = o.shape[1]
    pool = swapped[:, jw + kw + ow:jw + kw + ow + latent_cache.size].reshape((mp_size * latent_cache.shape[0],) + latent_cache.shape[1:])
    orr = swapped[:, jw + kw:jw + kw + ow].reshape(mp_size, 16, 64).transpose(1, 0, 2).reshape(16, mp_size * 64)
    jr = jnp.pad(jr, ((0, 0), (0, 3712 - 3648)))
    step_count, step_width = step_rows.shape
    step_block = jnp.pad(step_rows, ((0, 16 - step_count), (0, 128 - step_width)))
    block = jnp.concatenate([jr, orr, kr, step_block], axis=1)
    g = torus_gather(block, [0, 2304, 4608, 6912])
    w1 = g[:, :, :3648].reshape(2048, 3648)
    w3 = g[:, :, 3712:5760].reshape(2048, 2048)
    w2 = g[:, :, 5760:6784].reshape(128, 4, 4096).reshape(512, 4096)
    steps = lax.dynamic_slice_in_dim(g[:, :step_count, 6784:6784 + step_width], lax.axis_index("dp") * mp_size, mp_size, 0)
    steps = steps.transpose(1, 0, 2).reshape(step_count, mp_size * step_width)
    return w1, w2, w3, steps, pool


def rms_scale(values, scales):
    widened = values.astype(jnp.float32)
    mean_square = jnp.mean(widened * widened, axis=-1, keepdims=True)
    return widened * lax.rsqrt(mean_square + NORM_EPS) * scales


def rotate(values, positions):
    rot_width = values.shape[-1]
    half_width = rot_width // 2
    freq_steps = jnp.arange(half_width, dtype=jnp.float32)
    inv_freqs = jnp.exp(freq_steps * (-2.0 * math.log(ROPE_BASE) / rot_width))
    angles = positions.astype(jnp.float32)[:, None] * inv_freqs[None, :]
    angle_shape = (positions.shape[0],) + (1,) * (values.ndim - 2) + (half_width,)
    cosine = jnp.cos(angles).reshape(angle_shape)
    sine_part = jnp.sin(angles).reshape(angle_shape)
    lower_half = values[..., :half_width]
    upper_half = values[..., half_width:]
    return jnp.concatenate(
        [
            lower_half * cosine - upper_half * sine_part,
            upper_half * cosine + lower_half * sine_part,
        ],
        axis=-1,
    )


def queries_keys(projected, positions, latent_gain, up_heads):
    head_cols = H * (DN + DR)
    row_count = projected.shape[0]
    query_cols = projected[:, :head_cols].reshape(row_count, H, DN + DR)
    query_rot = rotate(query_cols[..., DN:].astype(jnp.float32), positions).astype(jnp.bfloat16)
    latent = rms_scale(projected[:, head_cols : head_cols + LAT], latent_gain).astype(jnp.bfloat16)
    key_rot = rotate(projected[:, head_cols + LAT :].astype(jnp.float32), positions).astype(
        jnp.bfloat16
    )
    query_lat = jnp.einsum(
        "rhn,lhn->rhl", query_cols[..., :DN], up_heads[:, 0], preferred_element_type=jnp.float32
    ).astype(jnp.bfloat16)
    return (query_lat, query_rot, latent, key_rot)


def prompt_attention(queries, query_ids, all_keys, all_ids, score_scale):
    row_count = queries[0].shape[0]
    block_rows = min(row_count, LEN // 2)
    outputs = []
    for start in range(0, row_count, block_rows):
        stop = start + block_rows
        key_start = start - start % LEN
        id_part, key_ids = query_ids[start:stop], all_ids[key_start:stop]
        latent_part = all_keys[0][key_start:stop]
        products = [
            jnp.einsum("qhc,kc->qhk", q[start:stop], k[key_start:stop], preferred_element_type=jnp.float32)
            for q, k in zip(queries, all_keys)
        ]
        scores = (products[0] + products[1]) * score_scale
        allowed = key_ids[None, :] <= id_part[:, None]
        scores = jnp.where(allowed[:, None, :], scores, MASKED)
        peak_score = jnp.max(scores, axis=-1, keepdims=True)
        weights = jnp.where(allowed[:, None, :], jnp.exp(scores - peak_score), 0.0)
        weight_sum = jnp.sum(weights, axis=-1, keepdims=True)
        summed = jnp.einsum(
            "qhk,kl->qhl",
            weights.astype(jnp.bfloat16),
            latent_part,
            preferred_element_type=jnp.float32,
        )
        outputs.append((summed / weight_sum).astype(jnp.bfloat16))
    return jnp.concatenate(outputs, axis=0)


def step_attention(queries, own_keys, pool, page_table, cached_lengths, score_scale):
    request_count, page_count = page_table.shape
    page_rows = pool.shape[1]
    pages = pool[page_table].reshape(request_count, page_count * page_rows, pool.shape[2])
    key_all = jnp.concatenate([pages, own_keys[:, None, :]], axis=1)
    cached_ok = (
        jnp.arange(page_count * page_rows, dtype=jnp.int32)[None, :] < cached_lengths[:, None]
    )
    allowed = jnp.concatenate([cached_ok, jnp.ones((request_count, 1), jnp.bool_)], axis=1)
    scores = (
        jnp.einsum("rhc,rkc->rhk", queries, key_all, preferred_element_type=jnp.float32)
        * score_scale
    )
    scores = jnp.where(allowed[:, None, :], scores, MASKED)
    peak_score = jnp.max(scores, axis=-1, keepdims=True)
    weights = jnp.where(allowed[:, None, :], jnp.exp(scores - peak_score), 0.0)
    weight_sum = jnp.sum(weights, axis=-1, keepdims=True)
    summed = jnp.einsum(
        "rhk,rkl->rhl",
        weights.astype(jnp.bfloat16),
        key_all[:, :, :LAT],
        preferred_element_type=jnp.float32,
    )
    return (summed / weight_sum).astype(jnp.bfloat16)


def on_device(
    prompt_rows,
    step_rows,
    attn_gain,
    latent_gain,
    joined_qkva,
    kv_up,
    out_proj,
    latent_cache,
    page_table,
    cached_lengths,
):
    prompt_count = prompt_rows.shape[0]
    mp_index = lax.axis_index("mp")
    mp_size = lax.axis_size("mp")
    score_scale = (DN + DR) ** (-0.5)
    *served, step_full, pool = gather_weights(joined_qkva, kv_up, out_proj, step_rows, latent_cache)
    stacked = jnp.concatenate([prompt_rows, step_full], axis=0)
    normed = rms_scale(stacked, attn_gain).astype(jnp.bfloat16)
    prompt_ids = jnp.arange(prompt_count, dtype=jnp.int32)
    positions = jnp.concatenate([prompt_ids % LEN, cached_lengths], axis=0)
    inputs = normed
    projected = jnp.dot(
        inputs,
        served[0],
        preferred_element_type=jnp.float32,
    )
    up_heads = served[1].reshape(LAT, 2, H, DN)
    query_lat, query_rot, latent, key_rot = queries_keys(
        projected.astype(jnp.bfloat16), positions, latent_gain, up_heads
    )
    step_queries = jnp.concatenate([query_lat[prompt_count:], query_rot[prompt_count:]], axis=-1)
    step_keys = jnp.concatenate([latent[prompt_count:], key_rot[prompt_count:]], axis=-1)
    prompt_latent = prompt_attention(
        (query_lat[:prompt_count], query_rot[:prompt_count]),
        prompt_ids,
        (latent[:prompt_count], key_rot[:prompt_count]),
        prompt_ids,
        score_scale,
    )
    step_latent = step_attention(
        step_queries, step_keys, pool, page_table, cached_lengths, score_scale
    )
    latent_out = jnp.concatenate([prompt_latent, step_latent], axis=0)
    heads_out = jnp.einsum(
        "rhl,lhv->rhv", latent_out, up_heads[:, 1], preferred_element_type=jnp.float32
    ).astype(jnp.bfloat16)
    heads_out = heads_out.reshape(latent_out.shape[0], H * DV)
    inputs = heads_out
    attended = jnp.dot(
        inputs,
        served[2],
        preferred_element_type=jnp.float32,
    )
    attended = attended.astype(jnp.bfloat16)
    prompt_out = attended[:prompt_count]
    col_width = attended.shape[1] // mp_size
    step_out = lax.dynamic_slice_in_dim(attended[prompt_count:], mp_index * col_width, col_width, 1)
    return (prompt_out, step_out)


def solution(mesh):
    placed = (
        P(("dp", "mp"), None),
        P("dp", "mp"),
        P(),
        P(),
        P("dp", "mp"),
        P("dp", "mp"),
        P("dp", "mp"),
        P(("dp", "mp"), None, None),
        P("dp", None),
        P("dp"),
    )
    return jax.shard_map(
        on_device,
        mesh=mesh,
        in_specs=placed,
        out_specs=(P(("dp", "mp"), None), P("dp", "mp")),
        check_vma=False,
    )
```

```python
import math

import numpy as np

import jax
import jax.numpy as jnp
from jax import lax
from jax.sharding import PartitionSpec as P

H = 16
DN = 128
DR = 64
DV = 128
LAT = 512
LEN = 512


NORM_EPS = 1e-06
ROPE_BASE = 50000.0
MASKED = -1e30


AXES = ("dp", "mp")


def _coords(i):
    dp, mp = i // 32, i % 32
    return (2 * (dp // 2) + (mp // 4) % 2, mp % 4, mp // 8, dp % 2)


def _index(x, y, z, core):
    return ((x // 2) * 2 + core) * 32 + z * 8 + (x % 2) * 4 + y


def _shift_pairs(dim, step):
    pairs = []
    for i in range(128):
        c = list(_coords(i))
        c[dim] = (c[dim] + step) % 4
        pairs.append((i, _index(*c)))
    return pairs


def torus_gather(block, cuts):
    rows = block.shape[0]
    me = lax.axis_index(AXES)
    dp, mp = me // 32, me % 32
    cx, cy, cz, ccore = 2 * (dp // 2) + (mp // 4) % 2, mp % 4, mp // 8, dp % 2
    ids = np.arange(128)
    x = 2 * (ids // 64) + (ids % 32 // 4) % 2
    y = ids % 4
    z = ids % 32 // 8
    core = (ids // 32) % 2
    rel = ((x - cx) % 4) * 16 + ((y - cy) % 4) * 4 + (z - cz) % 4
    pieces = []
    for part in range(len(cuts) - 1):
        data = block[:, cuts[part]:cuts[part + 1]]
        offs = [(0, 0, 0)]
        for stage in range(3):
            dim = (part + stage) % 3
            right = lax.ppermute(data, AXES, _shift_pairs(dim, 1))
            left = lax.ppermute(data, AXES, _shift_pairs(dim, -1))
            far = lax.ppermute(right, AXES, _shift_pairs(dim, 1))
            new_offs = list(offs)
            for delta in (-1, 1, -2):
                for o in offs:
                    o = list(o)
                    o[dim] = (o[dim] + delta) % 4
                    new_offs.append(tuple(o))
            data = jnp.concatenate([data, right, left, far], axis=0)
            offs = new_offs
        table = np.zeros((4, 4, 4), np.int32)
        for pos, o in enumerate(offs):
            table[o] = pos
        pick = jnp.take(jnp.asarray(table.reshape(-1)), rel, mode="clip") + (core - ccore) % 2 * 64
        partner = lax.ppermute(data, "dp", [(d, d ^ 1) for d in range(4)])
        slabs = jnp.concatenate([data, partner], axis=0).reshape(-1, rows, data.shape[-1])
        pieces.append(jnp.take(slabs, pick, axis=0, mode="clip"))
    return jnp.concatenate(pieces, axis=2)


def gather_weights(joined, kv_up, out_proj, step_rows, latent_cache):
    mp_size = 32
    j = joined.astype(jnp.bfloat16).reshape(mp_size, -1)
    k = kv_up.astype(jnp.bfloat16).reshape(mp_size, -1)
    o = out_proj.astype(jnp.bfloat16).reshape(mp_size, -1)
    cache = jnp.broadcast_to(latent_cache.reshape(1, -1), (mp_size, latent_cache.size))
    packed = jnp.concatenate([j, k, o, cache], axis=1)
    packed = jnp.pad(packed, ((0, 0), (0, -packed.shape[1] % 256)))
    swapped = lax.all_to_all(packed.reshape(mp_size, 2, -1), "mp", 0, 0, tiled=True)
    swapped = jnp.concatenate([swapped[:, 0], swapped[:, 1]], axis=1)
    jw, kw = j.shape[1], k.shape[1]
    jr = swapped[:, :jw].reshape(mp_size, 16, 114).transpose(1, 0, 2).reshape(16, mp_size * 114)
    kr = swapped[:, jw:jw + kw].reshape(mp_size // 2, 2, 4, 128).transpose(2, 1, 0, 3).reshape(16, 1024)
    ow = o.shape[1]
    pool = swapped[:, jw + kw + ow:jw + kw + ow + latent_cache.size].reshape((mp_size * latent_cache.shape[0],) + latent_cache.shape[1:])
    orr = swapped[:, jw + kw:jw + kw + ow].reshape(mp_size, 16, 64).transpose(1, 0, 2).reshape(16, mp_size * 64)
    jr = jnp.pad(jr, ((0, 0), (0, 3712 - 3648)))
    step_count, step_width = step_rows.shape
    step_block = jnp.pad(step_rows, ((0, 16 - step_count), (0, 128 - step_width)))
    block = jnp.concatenate([jr, orr, kr, step_block], axis=1)
    g = torus_gather(block, [0, 2304, 4608, 6912])
    w1 = g[:, :, :3648].reshape(2048, 3648)
    w3 = g[:, :, 3712:5760].reshape(2048, 2048)
    w2 = g[:, :, 5760:6784].reshape(128, 4, 4096).reshape(512, 4096)
    steps = lax.dynamic_slice_in_dim(g[:, :step_count, 6784:6784 + step_width], lax.axis_index("dp") * mp_size, mp_size, 0)
    steps = steps.transpose(1, 0, 2).reshape(step_count, mp_size * step_width)
    return w1, w2, w3, steps, pool


def rms_scale(values, scales):
    widened = values.astype(jnp.float32)
    mean_square = jnp.mean(widened * widened, axis=-1, keepdims=True)
    return widened * lax.rsqrt(mean_square + NORM_EPS) * scales


def rotate(values, positions):
    rot_width = values.shape[-1]
    half_width = rot_width // 2
    freq_steps = jnp.arange(half_width, dtype=jnp.float32)
    inv_freqs = jnp.exp(freq_steps * (-2.0 * math.log(ROPE_BASE) / rot_width))
    angles = positions.astype(jnp.float32)[:, None] * inv_freqs[None, :]
    angle_shape = (positions.shape[0],) + (1,) * (values.ndim - 2) + (half_width,)
    cosine = jnp.cos(angles).reshape(angle_shape)
    sine_part = jnp.sin(angles).reshape(angle_shape)
    lower_half = values[..., :half_width]
    upper_half = values[..., half_width:]
    return jnp.concatenate(
        [
            lower_half * cosine - upper_half * sine_part,
            upper_half * cosine + lower_half * sine_part,
        ],
        axis=-1,
    )


def queries_keys(projected, positions, latent_gain, up_heads):
    head_cols = H * (DN + DR)
    row_count = projected.shape[0]
    query_cols = projected[:, :head_cols].reshape(row_count, H, DN + DR)
    query_rot = rotate(query_cols[..., DN:].astype(jnp.float32), positions).astype(jnp.bfloat16)
    latent = rms_scale(projected[:, head_cols : head_cols + LAT], latent_gain).astype(jnp.bfloat16)
    key_rot = rotate(projected[:, head_cols + LAT :].astype(jnp.float32), positions).astype(
        jnp.bfloat16
    )
    query_lat = jnp.einsum(
        "rhn,lhn->rhl", query_cols[..., :DN], up_heads[:, 0], preferred_element_type=jnp.float32
    ).astype(jnp.bfloat16)
    return (query_lat, query_rot, latent, key_rot)


def prompt_attention(queries, query_ids, all_keys, all_ids, score_scale):
    row_count = queries[0].shape[0]
    block_rows = min(row_count, LEN // 2)
    outputs = []
    for start in range(0, row_count, block_rows):
        stop = start + block_rows
        key_start = start - start % LEN
        id_part, key_ids = query_ids[start:stop], all_ids[key_start:stop]
        latent_part = all_keys[0][key_start:stop]
        products = [
            jnp.einsum("qhc,kc->qhk", q[start:stop], k[key_start:stop], preferred_element_type=jnp.float32)
            for q, k in zip(queries, all_keys)
        ]
        scores = (products[0] + products[1]) * score_scale
        allowed = key_ids[None, :] <= id_part[:, None]
        scores = jnp.where(allowed[:, None, :], scores, MASKED)
        peak_score = jnp.max(scores, axis=-1, keepdims=True)
        weights = jnp.where(allowed[:, None, :], jnp.exp(scores - peak_score), 0.0)
        weight_sum = jnp.sum(weights, axis=-1, keepdims=True)
        summed = jnp.einsum(
            "qhk,kl->qhl",
            weights.astype(jnp.bfloat16),
            latent_part,
            preferred_element_type=jnp.float32,
        )
        outputs.append((summed / weight_sum).astype(jnp.bfloat16))
    return jnp.concatenate(outputs, axis=0)


def step_attention(queries, own_keys, pool, page_table, cached_lengths, score_scale):
    request_count, page_count = page_table.shape
    page_rows = pool.shape[1]
    pages = pool[page_table].reshape(request_count, page_count * page_rows, pool.shape[2])
    key_all = jnp.concatenate([pages, own_keys[:, None, :]], axis=1)
    cached_ok = (
        jnp.arange(page_count * page_rows, dtype=jnp.int32)[None, :] < cached_lengths[:, None]
    )
    allowed = jnp.concatenate([cached_ok, jnp.ones((request_count, 1), jnp.bool_)], axis=1)
    scores = (
        jnp.einsum("rhc,rkc->rhk", queries, key_all, preferred_element_type=jnp.float32)
        * score_scale
    )
    scores = jnp.where(allowed[:, None, :], scores, MASKED)
    peak_score = jnp.max(scores, axis=-1, keepdims=True)
    weights = jnp.where(allowed[:, None, :], jnp.exp(scores - peak_score), 0.0)
    weight_sum = jnp.sum(weights, axis=-1, keepdims=True)
    summed = jnp.einsum(
        "rhk,rkl->rhl",
        weights.astype(jnp.bfloat16),
        key_all[:, :, :LAT],
        preferred_element_type=jnp.float32,
    )
    return (summed / weight_sum).astype(jnp.bfloat16)


def on_device(
    prompt_rows,
    step_rows,
    attn_gain,
    latent_gain,
    joined_qkva,
    kv_up,
    out_proj,
    latent_cache,
    page_table,
    cached_lengths,
):
    prompt_count = prompt_rows.shape[0]
    mp_index = lax.axis_index("mp")
    mp_size = lax.axis_size("mp")
    score_scale = (DN + DR) ** (-0.5)
    *served, step_full, pool = gather_weights(joined_qkva, kv_up, out_proj, step_rows, latent_cache)
    stacked = jnp.concatenate([prompt_rows, step_full], axis=0)
    normed = rms_scale(stacked, attn_gain).astype(jnp.bfloat16)
    prompt_ids = jnp.arange(prompt_count, dtype=jnp.int32)
    positions = jnp.concatenate([prompt_ids % LEN, cached_lengths], axis=0)
    inputs = normed
    projected = jnp.dot(
        inputs,
        served[0],
        preferred_element_type=jnp.float32,
    )
    up_heads = served[1].reshape(LAT, 2, H, DN)
    query_lat, query_rot, latent, key_rot = queries_keys(
        projected.astype(jnp.bfloat16), positions, latent_gain, up_heads
    )
    step_queries = jnp.concatenate([query_lat[prompt_count:], query_rot[prompt_count:]], axis=-1)
    step_keys = jnp.concatenate([latent[prompt_count:], key_rot[prompt_count:]], axis=-1)
    prompt_latent = prompt_attention(
        (query_lat[:prompt_count], query_rot[:prompt_count]),
        prompt_ids,
        (latent[:prompt_count], key_rot[:prompt_count]),
        prompt_ids,
        score_scale,
    )
    step_latent = step_attention(
        step_queries, step_keys, pool, page_table, cached_lengths, score_scale
    )
    latent_out = jnp.concatenate([prompt_latent, step_latent], axis=0)
    heads_out = jnp.einsum(
        "rhl,lhv->rhv", latent_out, up_heads[:, 1], preferred_element_type=jnp.float32
    ).astype(jnp.bfloat16)
    heads_out = heads_out.reshape(latent_out.shape[0], H * DV)
    inputs = heads_out
    attended = jnp.dot(
        inputs,
        served[2],
        preferred_element_type=jnp.float32,
    )
    attended = attended.astype(jnp.bfloat16)
    prompt_out = attended[:prompt_count]
    col_width = attended.shape[1] // mp_size
    step_out = lax.dynamic_slice_in_dim(attended[prompt_count:], mp_index * col_width, col_width, 1)
    return (prompt_out, step_out)


def solution(mesh):
    placed = (
        P(("dp", "mp"), None),
        P("dp", "mp"),
        P(),
        P(),
        P("dp", "mp"),
        P("dp", "mp"),
        P("dp", "mp"),
        P(("dp", "mp"), None, None),
        P("dp", None),
        P("dp"),
    )
    return jax.shard_map(
        on_device,
        mesh=mesh,
        in_specs=placed,
        out_specs=(P(("dp", "mp"), None), P("dp", "mp")),
        check_vma=False,
    )
```
